512 devices in a mesh: row: 32 (over y, x), col: 16 (over z, core).
Axes of the slice: x: 4, y: 8, z: 8, core: 2. Of those that a mesh axis runs over, the one named last changes fastest.
Arguments:
- stored: float32 [8192, 8192], P('row', 'col'), as said below
Outputs:
- factored: float32 [8192, 8192], P('row', 'col')
Inputs may be any that keep to these rules, and one draw needn't show every extreme that they name: stored is the storage order of a symmetric positive definite matrix.
All inputs are finite; a program needn't handle non-finite values.
Results may differ from the reference program's by a relative error of at most 0.0001.
Values sent between devices are 32-bit elements; how exact they have to be, the bound alone decides.
No kernel may reach another device: no remote copies, remote signals or barrier semaphores. Data moves between devices by JAX's collectives and lax.ppermute only.
A program may use at most 64 MiB of HBM per device.

```python
import jax
import jax.numpy as jnp
from jax import lax

NB = 64
RB = 4
CB = 8
ORDER = 8192
N_ROW = 32
N_COL = 16


def draw_stored(key, part):
    key_noise = jax.random.fold_in(key, 11)
    key_diag = jax.random.fold_in(key, 12)
    noise = jax.random.normal(key_noise, (ORDER, ORDER), jnp.float32)
    symmetric = (noise + noise.T) * 0.7071
    shift_factor = jax.random.uniform(key_diag, (ORDER,), jnp.float32, 2.4, 2.9)
    extra = shift_factor * jnp.sqrt(jnp.float32(ORDER))
    positions = jnp.arange(ORDER, dtype=jnp.int32)
    on_diag = positions[:, None] == positions[None, :]
    kernel = jnp.where(on_diag, symmetric + extra[:, None], symmetric)
    return kernel.reshape(RB, N_ROW, NB, CB, N_COL, NB).transpose(1, 0, 2, 4, 3, 5).reshape(ORDER, ORDER)


def setup_inputs(seed: int = 0) -> dict:
    key_list = jax.random.split(jax.random.key(seed), 2)
    return {
        "stored": draw_stored(jax.random.fold_in(key_list[1], 71), 0),
    }


def reference(stored):
    matrix = stored.reshape(N_ROW, RB, NB, N_COL, CB, NB).transpose(1, 0, 2, 4, 3, 5).reshape(ORDER, ORDER)
    for panel_index in range(2):
        start = panel_index * NB
        finish = start + NB
        diag_factor = jnp.linalg.cholesky(matrix[start:finish, start:finish])
        below = matrix[finish:, start:finish]
        solved = jax.scipy.linalg.solve_triangular(diag_factor, below.T, lower=True).T
        matrix = matrix.at[finish:, finish:].add(-jnp.dot(solved.astype(jnp.float32), solved.T.astype(jnp.float32), precision=lax.Precision.HIGHEST, preferred_element_type=jnp.float32))
        column_new = jnp.concatenate([jnp.zeros((start, NB), jnp.float32), diag_factor, solved], axis=0)
        matrix = matrix.at[:, start:finish].set(column_new)
    block_ids = jnp.arange(ORDER, dtype=jnp.int32) // NB
    upper = (block_ids[:, None] < block_ids[None, :]) & (block_ids[None, :] >= 2)
    matrix = jnp.where(upper, jnp.zeros((), jnp.float32), matrix)
    return matrix.reshape(RB, N_ROW, NB, CB, N_COL, NB).transpose(1, 0, 2, 4, 3, 5).reshape(ORDER, ORDER)
```

```python
import jax
import jax.numpy as jnp
from jax import lax
from jax.sharding import PartitionSpec as P

NB = 64
HIGH = lax.Precision.HIGHEST


def both_axes(x, pairs):
    return lax.ppermute(x, ("row", "col"), pairs)


def gather_corner(stored, swapped, p, q, ncols):
    own = stored[:NB, :NB]
    got = swapped[:NB]
    d00, d01, d10, d11 = 0, 1, ncols, ncols + 1
    from_a = both_axes(own, [(d11, d00), (d00, d10)])
    from_b = both_axes(own, [(d11, d01), (d00, d11)])
    sent = jnp.where(q == 0, from_a, from_b)
    t = jnp.where(q == 0, got, own)
    u = jnp.where(q == 0, own, got)
    a00 = jnp.where(p == 0, u, sent)
    a10 = jnp.where(p == 0, t.T, u)
    a11 = jnp.where(p == 0, sent, t)
    return jnp.concatenate([a00, a10, a11], axis=0)


def spread_corner(corner, p, q, step, ncols):
    lin = lambda r, c: r * ncols + c
    src = [(r, c) for r in range(step) for c in range(step)]
    down = both_axes(corner, [(lin(r, c), lin(r + step, c)) for r, c in src])
    right = both_axes(corner, [(lin(r, c), lin(r, c + step)) for r, c in src])
    diag = both_axes(corner, [(lin(r, c), lin(r + step, c + step)) for r, c in src])
    low_p = (p >= step) & (p < 2 * step)
    low_q = (q >= step) & (q < 2 * step)
    top_p = p < step
    top_q = q < step
    out = jnp.where(low_p & top_q, down, corner)
    out = jnp.where(top_p & low_q, right, out)
    return jnp.where(low_p & low_q, diag, out)


def interleave(a, b, count):
    blocks = jnp.stack([a.reshape(count, NB, NB), b.reshape(count, NB, NB)], axis=1)
    return blocks.reshape(2 * count * NB, NB)


def solve_right(factor, rhs):
    return jax.scipy.linalg.solve_triangular(factor, rhs.T, lower=True).T


def per_device(stored):
    nrows = lax.axis_size("row")
    ncols = lax.axis_size("col")
    assert nrows == 2 * ncols
    half = nrows // 2
    p = lax.axis_index("row")
    q = lax.axis_index("col")
    row_count = stored.shape[0] // NB
    col_count = stored.shape[1] // NB
    assert col_count == 2 * row_count

    mine = stored[:, :NB]
    swapped = lax.ppermute(mine, "col", [(0, 1), (1, 0)])
    panel = jnp.concatenate(
        [jnp.where(q == 0, mine, swapped), jnp.where(q == 0, swapped, mine)], axis=0
    )
    corner = gather_corner(stored, swapped, p, q, ncols)
    step = 2
    while step < ncols:
        got = lax.ppermute(panel, "col", [(c, c + step) for c in range(step)])
        panel = jnp.where((q >= step) & (q < 2 * step), got, panel)
        corner = spread_corner(corner, p, q, step, ncols)
        step *= 2

    lin = lambda r, c: r * ncols + c
    carry = jnp.concatenate([panel, corner], axis=0)
    first_pairs = [(lin(c, r), lin(r, c)) for r in range(half) for c in range(ncols)]
    first_pairs += [(lin(c + half, r - half), lin(r, c)) for r in range(half, nrows) for c in range(ncols)]
    second_pairs = [(lin(c, r - half), lin(r, c)) for r in range(half, nrows) for c in range(ncols)]
    second_pairs += [(lin(c + half, r), lin(r, c)) for r in range(half) for c in range(ncols)]
    first = both_axes(carry, first_pairs)
    second = both_axes(carry, second_pairs)
    low = p < half
    near = jnp.where(low, first, second)
    far = jnp.where(low, second, first)
    rows_len = row_count * NB
    corner = near[2 * rows_len :]
    a00 = corner[:NB]
    a10 = corner[NB : 2 * NB]
    a11 = corner[2 * NB :]
    col0 = interleave(near[:rows_len], far[:rows_len], row_count)
    col1 = interleave(near[rows_len : 2 * rows_len], far[rows_len : 2 * rows_len], row_count)
    rows0 = panel[:rows_len]
    rows1 = panel[rows_len : 2 * rows_len]

    c0 = jnp.linalg.cholesky(a00)
    x = solve_right(c0, jnp.concatenate([a10, rows0, col0], axis=0))
    x1 = x[:NB]
    x_rest = x[NB:]
    c1 = jnp.linalg.cholesky(a11 - jnp.dot(x1, x1.T, precision=HIGH, preferred_element_type=jnp.float32))
    rest1 = jnp.concatenate([rows1, col1], axis=0)
    y = solve_right(c1, rest1 - jnp.dot(x_rest, x1.T, precision=HIGH, preferred_element_type=jnp.float32))
    w_rows = jnp.concatenate([x_rest[:rows_len], y[:rows_len]], axis=1)
    w_cols = jnp.concatenate([x_rest[rows_len:], y[rows_len:]], axis=1)
    update = jnp.dot(w_rows, w_cols.T, precision=HIGH, preferred_element_type=jnp.float32)

    row_ids = jnp.arange(row_count * NB, dtype=jnp.int32) // NB * nrows + p
    col_ids = jnp.arange(col_count * NB, dtype=jnp.int32) // NB * ncols + q
    keep = (col_ids[None, :] >= 2) & (row_ids[:, None] >= col_ids[None, :])
    result = jnp.where(keep, stored - update, 0.0)

    zero_block = jnp.zeros((NB, NB), jnp.float32)
    lead0 = jnp.concatenate([jnp.where(p == 0, c0, x_rest[:NB]), x_rest[NB:rows_len]], axis=0)
    lead1_top = jnp.where(p == 0, zero_block, jnp.where(p == 1, c1, y[:NB]))
    lead1 = jnp.concatenate([lead1_top, y[NB:rows_len]], axis=0)
    lead = jnp.where(q == 0, lead0, lead1)
    head = jnp.where(q < 2, lead, result[:, :NB])
    return jnp.concatenate([head, result[:, NB:]], axis=1)


def solution(mesh):
    return jax.shard_map(
        per_device,
        mesh=mesh,
        in_specs=(P("row", "col"),),
        out_specs=P("row", "col"),
        check_vma=False,
    )
```

```python
import jax
import jax.numpy as jnp
import numpy as np
from jax import lax
from jax.sharding import PartitionSpec as P

NB = 64
HIGH = lax.Precision.HIGHEST


def both_axes(x, pairs):
    return lax.ppermute(x, ("row", "col"), pairs)


def mm(a, b):
    return jnp.dot(a, b, precision=HIGH, preferred_element_type=jnp.float32)


def gather_corner(stored, swapped, p, q, ncols):
    own = stored[:NB, :NB]
    got = swapped[:NB]
    d00, d01, d10, d11 = 0, 1, ncols, ncols + 1
    from_a = both_axes(own, [(d11, d00), (d00, d10)])
    from_b = both_axes(own, [(d11, d01), (d00, d11)])
    sent = jnp.where(q == 0, from_a, from_b)
    t = jnp.where(q == 0, got, own)
    u = jnp.where(q == 0, own, got)
    a00 = jnp.where(p == 0, u, sent)
    a10 = jnp.where(p == 0, t.T, u)
    a11 = jnp.where(p == 0, sent, t)
    return jnp.concatenate([a00, a10, a11], axis=0)


def spread_round(value, holders, offsets, p, q, nrows, ncols):
    pick = np.full((nrows, ncols), -1, np.int32)
    received = []
    grown = set(holders)
    for k, (dr, dc) in enumerate(offsets):
        pairs = []
        for r, c in sorted(holders):
            pairs.append((r * ncols + c, (r + dr) * ncols + c + dc))
            pick[r + dr, c + dc] = k
            grown.add((r + dr, c + dc))
        received.append(both_axes(value, pairs))
    choice = jnp.asarray(pick)[p, q]
    for k, got in enumerate(received):
        value = jnp.where(choice == k, got, value)
    return value, grown


def interleave(a, b, count):
    blocks = jnp.stack([a.reshape(count, NB, NB), b.reshape(count, NB, NB)], axis=1)
    return blocks.reshape(2 * count * NB, NB)


def lower_inverse(factor):
    eye = jnp.eye(NB, dtype=jnp.float32)
    return jax.scipy.linalg.solve_triangular(factor, eye, lower=True)


def per_device(stored):
    nrows = lax.axis_size("row")
    ncols = lax.axis_size("col")
    assert nrows == 2 * ncols and ncols == 16
    half = nrows // 2
    p = lax.axis_index("row")
    q = lax.axis_index("col")
    row_count = stored.shape[0] // NB
    col_count = stored.shape[1] // NB
    assert col_count == 2 * row_count
    rows_len = row_count * NB

    mine = stored[:, :NB]
    swapped = lax.ppermute(mine, "col", [(0, 1), (1, 0)])
    panel = jnp.concatenate(
        [jnp.where(q == 0, mine, swapped), jnp.where(q == 0, swapped, mine)], axis=0
    )
    corner = gather_corner(stored, swapped, p, q, ncols)

    holders_col = [0, 1]
    holders_k = {(0, 0), (0, 1), (1, 0), (1, 1)}
    corner_offsets = [
        [(a * 16 + b * 8, c * 8) for a in (0, 1) for b in (0, 1) for c in (0, 1)][1:],
        [(4, 0), (0, 4), (4, 4)],
        [(2, 0), (0, 2), (2, 2)],
    ]
    for step, offsets in zip((8, 4, 2), corner_offsets):
        got = lax.ppermute(panel, "col", [(c, c + step) for c in holders_col])
        reached = np.zeros((ncols,), bool)
        reached[[c + step for c in holders_col]] = True
        panel = jnp.where(jnp.asarray(reached)[q], got, panel)
        holders_col = holders_col + [c + step for c in holders_col]
        corner, holders_k = spread_round(corner, holders_k, offsets, p, q, nrows, ncols)

    lin = lambda r, c: r * ncols + c
    first_pairs = [(lin(c, r), lin(r, c)) for r in range(half) for c in range(ncols)]
    first_pairs += [(lin(c + half, r - half), lin(r, c)) for r in range(half, nrows) for c in range(ncols)]
    second_pairs = [(lin(c, r - half), lin(r, c)) for r in range(half, nrows) for c in range(ncols)]
    second_pairs += [(lin(c + half, r), lin(r, c)) for r in range(half) for c in range(ncols)]
    first = both_axes(panel, first_pairs)
    second = both_axes(panel, second_pairs)

    a00 = corner[:NB]
    a10 = corner[NB : 2 * NB]
    a11 = corner[2 * NB :]
    rows0 = panel[:rows_len]
    rows1 = panel[rows_len:]
    c0 = jnp.linalg.cholesky(a00)
    inv0_t = lower_inverse(c0).T
    x1 = mm(a10, inv0_t)
    c1 = jnp.linalg.cholesky(a11 - mm(x1, x1.T))
    inv1_t = lower_inverse(c1).T
    x_rows = mm(rows0, inv0_t)
    y_rows = mm(rows1 - mm(x_rows, x1.T), inv1_t)
    cross = -mm(mm(inv0_t, x1.T), inv1_t)
    zero_block = jnp.zeros((NB, NB), jnp.float32)
    h = jnp.concatenate(
        [jnp.concatenate([inv0_t, cross], axis=1), jnp.concatenate([zero_block, inv1_t], axis=1)], axis=0
    )
    w_rows = jnp.concatenate([x_rows, y_rows], axis=1)
    v = mm(w_rows, h.T)

    low = p < half
    near = jnp.where(low, first, second)
    far = jnp.where(low, second, first)
    col0 = interleave(near[:rows_len], far[:rows_len], row_count)
    col1 = interleave(near[rows_len:], far[rows_len:], row_count)
    cols = jnp.concatenate([col0, col1], axis=1)
    update = mm(v, cols.T)

    row_ids = jnp.arange(row_count * NB, dtype=jnp.int32) // NB * nrows + p
    col_ids = jnp.arange(col_count * NB, dtype=jnp.int32) // NB * ncols + q
    keep = (col_ids[None, :] >= 2) & (row_ids[:, None] >= col_ids[None, :])
    result = jnp.where(keep, stored - update, 0.0)

    lead0 = jnp.concatenate([jnp.where(p == 0, c0, x_rows[:NB]), x_rows[NB:]], axis=0)
    lead1_top = jnp.where(p == 0, zero_block, jnp.where(p == 1, c1, y_rows[:NB]))
    lead1 = jnp.concatenate([lead1_top, y_rows[NB:]], axis=0)
    lead = jnp.where(q == 0, lead0, lead1)
    head = jnp.where(q < 2, lead, result[:, :NB])
    return jnp.concatenate([head, result[:, NB:]], axis=1)


def solution(mesh):
    return jax.shard_map(
        per_device,
        mesh=mesh,
        in_specs=(P("row", "col"),),
        out_specs=P("row", "col"),
        check_vma=False,
    )
```

```python
import jax
import jax.numpy as jnp
from jax import lax
from jax.sharding import PartitionSpec as P

NB = 64
HIGH = lax.Precision.HIGHEST


def both_axes(x, pairs):
    return lax.ppermute(x, ("row", "col"), pairs)


def mm(a, b):
    return jnp.dot(a, b, precision=HIGH, preferred_element_type=jnp.float32)


def gather_corner(stored, swapped, p, q, ncols):
    own = stored[:NB, :NB]
    got = swapped[:NB]
    d00, d01, d10, d11 = 0, 1, ncols, ncols + 1
    from_a = both_axes(own, [(d11, d00), (d00, d10)])
    from_b = both_axes(own, [(d11, d01), (d00, d11)])
    sent = jnp.where(q == 0, from_a, from_b)
    t = jnp.where(q == 0, got, own)
    u = jnp.where(q == 0, own, got)
    a00 = jnp.where(p == 0, u, sent)
    a10 = jnp.where(p == 0, t.T, u)
    a11 = jnp.where(p == 0, sent, t)
    return jnp.concatenate([a00, a10, a11], axis=0)


def spread_round(value, holders, offsets, ncols):
    grown = set(holders)
    total = value
    for dr, dc in offsets:
        pairs = [(r * ncols + c, (r + dr) * ncols + c + dc) for r, c in sorted(holders)]
        total = total + both_axes(value, pairs)
        grown.update((r + dr, c + dc) for r, c in holders)
    return total, grown


def interleave(a, b, count):
    blocks = jnp.stack([a.reshape(count, NB, NB), b.reshape(count, NB, NB)], axis=1)
    return blocks.reshape(2 * count * NB, NB)


def lower_inverse(factor):
    eye = jnp.eye(NB, dtype=jnp.float32)
    return jax.scipy.linalg.solve_triangular(factor, eye, lower=True)


def per_device(stored):
    nrows = lax.axis_size("row")
    ncols = lax.axis_size("col")
    assert nrows == 2 * ncols and ncols == 16
    half = nrows // 2
    p = lax.axis_index("row")
    q = lax.axis_index("col")
    row_count = stored.shape[0] // NB
    col_count = stored.shape[1] // NB
    assert col_count == 2 * row_count
    rows_len = row_count * NB

    mine = stored[:, :NB]
    swapped = lax.ppermute(mine, "col", [(0, 1), (1, 0)])
    panel = jnp.concatenate(
        [jnp.where(q == 0, mine, swapped), jnp.where(q == 0, swapped, mine)], axis=0
    )
    panel = jnp.where(q < 2, panel, 0.0)
    corner = jnp.where((p < 2) & (q < 2), gather_corner(stored, swapped, p, q, ncols), 0.0)

    holders_col = [0, 1]
    holders_k = {(0, 0), (0, 1), (1, 0), (1, 1)}
    corner_offsets = [
        [(a * 16 + b * 8, c * 8) for a in (0, 1) for b in (0, 1) for c in (0, 1)][1:],
        [(4, 0), (0, 4), (4, 4)],
        [(2, 0), (0, 2), (2, 2)],
    ]
    for step, offsets in zip((8, 4, 2), corner_offsets):
        panel = panel + lax.ppermute(panel, "col", [(c, c + step) for c in holders_col])
        holders_col = holders_col + [c + step for c in holders_col]
        corner, holders_k = spread_round(corner, holders_k, offsets, ncols)
    corner, panel = lax.optimization_barrier((corner, panel))

    lin = lambda r, c: r * ncols + c
    first_pairs = [(lin(c, r), lin(r, c)) for r in range(half) for c in range(ncols)]
    first_pairs += [(lin(c + half, r - half), lin(r, c)) for r in range(half, nrows) for c in range(ncols)]
    second_pairs = [(lin(c, r - half), lin(r, c)) for r in range(half, nrows) for c in range(ncols)]
    second_pairs += [(lin(c + half, r), lin(r, c)) for r in range(half) for c in range(ncols)]
    first = both_axes(panel, first_pairs)
    second = both_axes(panel, second_pairs)

    a00 = corner[:NB]
    a10 = corner[NB : 2 * NB]
    a11 = corner[2 * NB :]
    rows0 = panel[:rows_len]
    rows1 = panel[rows_len:]
    c0 = jnp.linalg.cholesky(a00)
    inv0_t = lower_inverse(c0).T
    x1 = mm(a10, inv0_t)
    c1 = jnp.linalg.cholesky(a11 - mm(x1, x1.T))
    inv1_t = lower_inverse(c1).T
    x_rows = mm(rows0, inv0_t)
    y_rows = mm(rows1 - mm(x_rows, x1.T), inv1_t)
    cross = -mm(mm(inv0_t, x1.T), inv1_t)
    zero_block = jnp.zeros((NB, NB), jnp.float32)
    h = jnp.concatenate(
        [jnp.concatenate([inv0_t, cross], axis=1), jnp.concatenate([zero_block, inv1_t], axis=1)], axis=0
    )
    w_rows = jnp.concatenate([x_rows, y_rows], axis=1)
    v = mm(w_rows, h.T)

    low = p < half
    near = jnp.where(low, first, second)
    far = jnp.where(low, second, first)
    col0 = interleave(near[:rows_len], far[:rows_len], row_count)
    col1 = interleave(near[rows_len:], far[rows_len:], row_count)
    cols = jnp.concatenate([col0, col1], axis=1)
    update = mm(v, cols.T)

    row_ids = jnp.arange(row_count * NB, dtype=jnp.int32) // NB * nrows + p
    col_ids = jnp.arange(col_count * NB, dtype=jnp.int32) // NB * ncols + q
    keep = (col_ids[None, :] >= 2) & (row_ids[:, None] >= col_ids[None, :])
    result = jnp.where(keep, stored - update, 0.0)

    lead0 = jnp.concatenate([jnp.where(p == 0, c0, x_rows[:NB]), x_rows[NB:]], axis=0)
    lead1_top = jnp.where(p == 0, zero_block, jnp.where(p == 1, c1, y_rows[:NB]))
    lead1 = jnp.concatenate([lead1_top, y_rows[NB:]], axis=0)
    lead = jnp.where(q == 0, lead0, lead1)
    head = jnp.where(q < 2, lead, result[:, :NB])
    return jnp.concatenate([head, result[:, NB:]], axis=1)


def solution(mesh):
    return jax.shard_map(
        per_device,
        mesh=mesh,
        in_specs=(P("row", "col"),),
        out_specs=P("row", "col"),
        check_vma=False,
    )
```

```python
import jax
import jax.numpy as jnp
from jax import lax
from jax.sharding import PartitionSpec as P

NB = 64
HIGH = lax.Precision.HIGHEST


def both_axes(x, pairs):
    return lax.ppermute(x, ("row", "col"), pairs)


def mm(a, b):
    return jnp.dot(a, b, precision=HIGH, preferred_element_type=jnp.float32)


def gather_corner(stored, swapped, p, q, ncols):
    own = stored[:NB, :NB]
    got = swapped[:NB]
    d00, d01, d10, d11 = 0, 1, ncols, ncols + 1
    from_a = both_axes(own, [(d11, d00), (d00, d10)])
    from_b = both_axes(own, [(d11, d01), (d00, d11)])
    sent = jnp.where(q == 0, from_a, from_b)
    t = jnp.where(q == 0, got, own)
    u = jnp.where(q == 0, own, got)
    a00 = jnp.where(p == 0, u, sent)
    a10 = jnp.where(p == 0, t.T, u)
    a11 = jnp.where(p == 0, sent, t)
    return jnp.concatenate([a00, a10, a11], axis=0)


def spread_round(value, holders, offsets, ncols):
    grown = set(holders)
    total = value
    for dr, dc in offsets:
        pairs = [(r * ncols + c, (r + dr) * ncols + c + dc) for r, c in sorted(holders)]
        total = total + both_axes(value, pairs)
        grown.update((r + dr, c + dc) for r, c in holders)
    return total, grown


def interleave(a, b, count):
    blocks = jnp.stack([a.reshape(count, NB, NB), b.reshape(count, NB, NB)], axis=1)
    return blocks.reshape(2 * count * NB, NB)


def lower_inverse(factor):
    eye = jnp.eye(factor.shape[0], dtype=jnp.float32)
    return jax.scipy.linalg.solve_triangular(factor, eye, lower=True)


def per_device(stored):
    nrows = lax.axis_size("row")
    ncols = lax.axis_size("col")
    assert nrows == 2 * ncols and ncols == 16
    half = nrows // 2
    p = lax.axis_index("row")
    q = lax.axis_index("col")
    row_count = stored.shape[0] // NB
    col_count = stored.shape[1] // NB
    assert col_count == 2 * row_count
    rows_len = row_count * NB

    mine = stored[:, :NB]
    swapped = lax.ppermute(mine, "col", [(0, 1), (1, 0)])
    panel = jnp.concatenate(
        [jnp.where(q == 0, mine, swapped), jnp.where(q == 0, swapped, mine)], axis=0
    )
    panel = jnp.where(q < 2, panel, 0.0)
    corner = jnp.where((p < 2) & (q < 2), gather_corner(stored, swapped, p, q, ncols), 0.0)

    holders_col = [0, 1]
    holders_k = {(0, 0), (0, 1), (1, 0), (1, 1)}
    corner_offsets = [
        [(a * 16 + b * 8, c * 8) for a in (0, 1) for b in (0, 1) for c in (0, 1)][1:],
        [(4, 0), (0, 4), (4, 4)],
        [(2, 0), (0, 2), (2, 2)],
    ]
    for step, offsets in zip((8, 4, 2), corner_offsets):
        panel = panel + lax.ppermute(panel, "col", [(c, c + step) for c in holders_col])
        holders_col = holders_col + [c + step for c in holders_col]
        corner, holders_k = spread_round(corner, holders_k, offsets, ncols)
    corner, panel = lax.optimization_barrier((corner, panel))

    lin = lambda r, c: r * ncols + c
    first_pairs = [(lin(c, r), lin(r, c)) for r in range(half) for c in range(ncols)]
    first_pairs += [(lin(c + half, r - half), lin(r, c)) for r in range(half, nrows) for c in range(ncols)]
    second_pairs = [(lin(c, r - half), lin(r, c)) for r in range(half, nrows) for c in range(ncols)]
    second_pairs += [(lin(c + half, r), lin(r, c)) for r in range(half) for c in range(ncols)]
    first = both_axes(panel, first_pairs)
    second = both_axes(panel, second_pairs)

    a00 = corner[:NB]
    a10 = corner[NB : 2 * NB]
    a11 = corner[2 * NB :]
    lead_block = jnp.concatenate(
        [jnp.concatenate([a00, a10.T], axis=1), jnp.concatenate([a10, a11], axis=1)], axis=0
    )
    factor = jnp.linalg.cholesky(lead_block)
    inv_t = lower_inverse(factor).T
    c0 = factor[:NB, :NB]
    c1 = factor[NB:, NB:]
    w_rows = mm(jnp.concatenate([panel[:rows_len], panel[rows_len:]], axis=1), inv_t)
    x_rows = w_rows[:, :NB]
    y_rows = w_rows[:, NB:]
    v = mm(w_rows, inv_t.T)
    zero_block = jnp.zeros((NB, NB), jnp.float32)

    low = p < half
    near = jnp.where(low, first, second)
    far = jnp.where(low, second, first)
    col0 = interleave(near[:rows_len], far[:rows_len], row_count)
    col1 = interleave(near[rows_len:], far[rows_len:], row_count)
    cols = jnp.concatenate([col0, col1], axis=1)
    update = mm(v, cols.T)

    row_ids = jnp.arange(row_count * NB, dtype=jnp.int32) // NB * nrows + p
    col_ids = jnp.arange(col_count * NB, dtype=jnp.int32) // NB * ncols + q
    keep = (col_ids[None, :] >= 2) & (row_ids[:, None] >= col_ids[None, :])
    result = jnp.where(keep, stored - update, 0.0)

    lead0 = jnp.concatenate([jnp.where(p == 0, c0, x_rows[:NB]), x_rows[NB:]], axis=0)
    lead1_top = jnp.where(p == 0, zero_block, jnp.where(p == 1, c1, y_rows[:NB]))
    lead1 = jnp.concatenate([lead1_top, y_rows[NB:]], axis=0)
    lead = jnp.where(q == 0, lead0, lead1)
    head = jnp.where(q < 2, lead, result[:, :NB])
    return jnp.concatenate([head, result[:, NB:]], axis=1)


def solution(mesh):
    return jax.shard_map(
        per_device,
        mesh=mesh,
        in_specs=(P("row", "col"),),
        out_specs=P("row", "col"),
        check_vma=False,
    )
```

```python
import jax
import jax.numpy as jnp
from jax import lax
from jax.sharding import PartitionSpec as P

NB = 64
HIGH = lax.Precision.HIGHEST


def both_axes(x, pairs):
    return lax.ppermute(x, ("row", "col"), pairs)


def mm(a, b):
    return jnp.dot(a, b, precision=HIGH, preferred_element_type=jnp.float32)


def gather_corner(stored, swapped, p, q, ncols):
    own = stored[:NB, :NB]
    got = swapped[:NB]
    d00, d01, d10, d11 = 0, 1, ncols, ncols + 1
    from_a = both_axes(own, [(d11, d00), (d00, d10)])
    from_b = both_axes(own, [(d11, d01), (d00, d11)])
    sent = jnp.where(q == 0, from_a, from_b)
    t = jnp.where(q == 0, got, own)
    u = jnp.where(q == 0, own, got)
    a00 = jnp.where(p == 0, u, sent)
    a10 = jnp.where(p == 0, t.T, u)
    a11 = jnp.where(p == 0, sent, t)
    return jnp.concatenate([a00, a10, a11], axis=0)


def spread_round(value, holders, offsets, ncols):
    grown = set(holders)
    total = value
    for dr, dc in offsets:
        pairs = [(r * ncols + c, (r + dr) * ncols + c + dc) for r, c in sorted(holders)]
        total = total + both_axes(value, pairs)
        grown.update((r + dr, c + dc) for r, c in holders)
    return total, grown


def interleave(a, b, count):
    blocks = jnp.stack([a.reshape(count, NB, NB), b.reshape(count, NB, NB)], axis=1)
    return blocks.reshape(2 * count * NB, NB)


def lower_inverse(factor):
    eye = jnp.eye(factor.shape[0], dtype=jnp.float32)
    return jax.scipy.linalg.solve_triangular(factor, eye, lower=True)


def per_device(stored):
    nrows = lax.axis_size("row")
    ncols = lax.axis_size("col")
    assert nrows == 2 * ncols and ncols == 16
    half = nrows // 2
    p = lax.axis_index("row")
    q = lax.axis_index("col")
    row_count = stored.shape[0] // NB
    col_count = stored.shape[1] // NB
    assert col_count == 2 * row_count
    rows_len = row_count * NB

    mine = stored[:, :NB]
    swapped = lax.ppermute(mine, "col", [(0, 1), (1, 0)])
    panel = jnp.concatenate(
        [jnp.where(q == 0, mine, swapped), jnp.where(q == 0, swapped, mine)], axis=0
    )
    panel = jnp.where(q < 2, panel, 0.0)
    corner = jnp.where((p < 2) & (q < 2), gather_corner(stored, swapped, p, q, ncols), 0.0)

    sent = panel
    for t in range((ncols - 2) // 2):
        panel = panel + lax.ppermute(sent, "col", [(0, 2 + 2 * t), (1, 3 + 2 * t)])
    holders_k = {(0, 0), (0, 1), (1, 0), (1, 1)}
    corner_offsets = [
        [(16, 0), (0, 8), (16, 8)],
        [(a * 8 + b * 4, c * 4) for a in (0, 1) for b in (0, 1) for c in (0, 1)][1:],
        [(2, 0), (0, 2), (2, 2)],
    ]
    for offsets in corner_offsets:
        corner, holders_k = spread_round(corner, holders_k, offsets, ncols)
    assert len(holders_k) == nrows * ncols

    lin = lambda r, c: r * ncols + c
    first_pairs = [(lin(c, r), lin(r, c)) for r in range(half) for c in range(ncols)]
    first_pairs += [(lin(c + half, r - half), lin(r, c)) for r in range(half, nrows) for c in range(ncols)]
    second_pairs = [(lin(c, r - half), lin(r, c)) for r in range(half, nrows) for c in range(ncols)]
    second_pairs += [(lin(c + half, r), lin(r, c)) for r in range(half) for c in range(ncols)]
    first = both_axes(panel, first_pairs)
    second = both_axes(panel, second_pairs)

    a00 = corner[:NB]
    a10 = corner[NB : 2 * NB]
    a11 = corner[2 * NB :]
    lead_block = jnp.concatenate(
        [jnp.concatenate([a00, a10.T], axis=1), jnp.concatenate([a10, a11], axis=1)], axis=0
    )
    factor = jnp.linalg.cholesky(lead_block)
    inv_t = lower_inverse(factor).T
    c0 = factor[:NB, :NB]
    c1 = factor[NB:, NB:]
    w_rows = mm(jnp.concatenate([panel[:rows_len], panel[rows_len:]], axis=1), inv_t)
    x_rows = w_rows[:, :NB]
    y_rows = w_rows[:, NB:]
    v = mm(w_rows, inv_t.T)
    zero_block = jnp.zeros((NB, NB), jnp.float32)

    low = p < half
    near = jnp.where(low, first, second)
    far = jnp.where(low, second, first)
    col0 = interleave(near[:rows_len], far[:rows_len], row_count)
    col1 = interleave(near[rows_len:], far[rows_len:], row_count)
    cols = jnp.concatenate([col0, col1], axis=1)
    update = mm(v, cols.T)

    row_ids = jnp.arange(row_count * NB, dtype=jnp.int32) // NB * nrows + p
    col_ids = jnp.arange(col_count * NB, dtype=jnp.int32) // NB * ncols + q
    keep = (col_ids[None, :] >= 2) & (row_ids[:, None] >= col_ids[None, :])
    result = jnp.where(keep, stored - update, 0.0)

    lead0 = jnp.concatenate([jnp.where(p == 0, c0, x_rows[:NB]), x_rows[NB:]], axis=0)
    lead1_top = jnp.where(p == 0, zero_block, jnp.where(p == 1, c1, y_rows[:NB]))
    lead1 = jnp.concatenate([lead1_top, y_rows[NB:]], axis=0)
    lead = jnp.where(q == 0, lead0, lead1)
    head = jnp.where(q < 2, lead, result[:, :NB])
    return jnp.concatenate([head, result[:, NB:]], axis=1)


def solution(mesh):
    return jax.shard_map(
        per_device,
        mesh=mesh,
        in_specs=(P("row", "col"),),
        out_specs=P("row", "col"),
        check_vma=False,
    )
```

```python
import jax
import jax.numpy as jnp
from jax import lax
from jax.sharding import PartitionSpec as P

NB = 64
HIGH = lax.Precision.HIGHEST


def both_axes(x, pairs):
    return lax.ppermute(x, ("row", "col"), pairs)


def mm(a, b):
    return jnp.dot(a, b, precision=HIGH, preferred_element_type=jnp.float32)


def gather_corner(stored, swapped, p, q, ncols):
    own = stored[:NB, :NB]
    got = swapped[:NB]
    d00, d01, d10, d11 = 0, 1, ncols, ncols + 1
    from_a = both_axes(own, [(d11, d00), (d00, d10)])
    from_b = both_axes(own, [(d11, d01), (d00, d11)])
    sent = jnp.where(q == 0, from_a, from_b)
    t = jnp.where(q == 0, got, own)
    u = jnp.where(q == 0, own, got)
    a00 = jnp.where(p == 0, u, sent)
    a10 = jnp.where(p == 0, t.T, u)
    a11 = jnp.where(p == 0, sent, t)
    return jnp.concatenate([a00, a10, a11], axis=0)


def spread_round(value, holders, offsets, ncols):
    grown = set(holders)
    total = value
    for dr, dc in offsets:
        pairs = [(r * ncols + c, (r + dr) * ncols + c + dc) for r, c in sorted(holders)]
        total = total + both_axes(value, pairs)
        grown.update((r + dr, c + dc) for r, c in holders)
    return total, grown


def interleave(a, b, count):
    blocks = jnp.stack([a.reshape(count, NB, NB), b.reshape(count, NB, NB)], axis=1)
    return blocks.reshape(2 * count * NB, NB)


def lower_inverse(factor):
    eye = jnp.eye(factor.shape[0], dtype=jnp.float32)
    return jax.scipy.linalg.solve_triangular(factor, eye, lower=True)


def per_device(stored):
    nrows = lax.axis_size("row")
    ncols = lax.axis_size("col")
    assert nrows == 2 * ncols and ncols == 16
    half = nrows // 2
    p = lax.axis_index("row")
    q = lax.axis_index("col")
    row_count = stored.shape[0] // NB
    col_count = stored.shape[1] // NB
    assert col_count == 2 * row_count
    rows_len = row_count * NB

    mine = stored[:, :NB]
    swapped = lax.ppermute(mine, "col", [(0, 1), (1, 0)])
    panel = jnp.concatenate(
        [jnp.where(q == 0, mine, swapped), jnp.where(q == 0, swapped, mine)], axis=0
    )
    panel = jnp.where(q < 2, panel, 0.0)
    corner = jnp.where((p < 2) & (q < 2), gather_corner(stored, swapped, p, q, ncols), 0.0)

    holders_col = [0, 1]
    holders_k = {(0, 0), (0, 1), (1, 0), (1, 1)}
    corner_offsets = [
        [(a * 16 + b * 8, c * 8) for a in (0, 1) for b in (0, 1) for c in (0, 1)][1:],
        [(4, 0), (0, 4), (4, 4)],
        [(2, 0), (0, 2), (2, 2)],
    ]
    for step, offsets in zip((8, 4, 2), corner_offsets):
        panel = panel + lax.ppermute(panel, "col", [(c, c + step) for c in holders_col])
        holders_col = holders_col + [c + step for c in holders_col]
        if step == 2:
            corner, panel = lax.optimization_barrier((corner, panel))
        corner, holders_k = spread_round(corner, holders_k, offsets, ncols)
    corner, panel_held = lax.optimization_barrier((corner, panel))

    lin = lambda r, c: r * ncols + c
    first_pairs = [(lin(c, r), lin(r, c)) for r in range(half) for c in range(ncols)]
    first_pairs += [(lin(c + half, r - half), lin(r, c)) for r in range(half, nrows) for c in range(ncols)]
    second_pairs = [(lin(c, r - half), lin(r, c)) for r in range(half, nrows) for c in range(ncols)]
    second_pairs += [(lin(c + half, r), lin(r, c)) for r in range(half) for c in range(ncols)]
    first = both_axes(panel, first_pairs)
    second = both_axes(panel, second_pairs)

    a00 = corner[:NB]
    a10 = corner[NB : 2 * NB]
    a11 = corner[2 * NB :]
    lead_block = jnp.concatenate(
        [jnp.concatenate([a00, a10.T], axis=1), jnp.concatenate([a10, a11], axis=1)], axis=0
    )
    factor = jnp.linalg.cholesky(lead_block)
    inv_t = lower_inverse(factor).T
    c0 = factor[:NB, :NB]
    c1 = factor[NB:, NB:]
    w_rows = mm(jnp.concatenate([panel_held[:rows_len], panel_held[rows_len:]], axis=1), inv_t)
    x_rows = w_rows[:, :NB]
    y_rows = w_rows[:, NB:]
    v = mm(w_rows, inv_t.T)
    zero_block = jnp.zeros((NB, NB), jnp.float32)

    low = p < half
    near = jnp.where(low, first, second)
    far = jnp.where(low, second, first)
    col0 = interleave(near[:rows_len], far[:rows_len], row_count)
    col1 = interleave(near[rows_len:], far[rows_len:], row_count)
    cols = jnp.concatenate([col0, col1], axis=1)
    update = mm(v, cols.T)

    row_ids = jnp.arange(row_count * NB, dtype=jnp.int32) // NB * nrows + p
    col_ids = jnp.arange(col_count * NB, dtype=jnp.int32) // NB * ncols + q
    keep = (col_ids[None, :] >= 2) & (row_ids[:, None] >= col_ids[None, :])
    result = jnp.where(keep, stored - update, 0.0)

    lead0 = jnp.concatenate([jnp.where(p == 0, c0, x_rows[:NB]), x_rows[NB:]], axis=0)
    lead1_top = jnp.where(p == 0, zero_block, jnp.where(p == 1, c1, y_rows[:NB]))
    lead1 = jnp.concatenate([lead1_top, y_rows[NB:]], axis=0)
    lead = jnp.where(q == 0, lead0, lead1)
    head = jnp.where(q < 2, lead, result[:, :NB])
    return jnp.concatenate([head, result[:, NB:]], axis=1)


def solution(mesh):
    return jax.shard_map(
        per_device,
        mesh=mesh,
        in_specs=(P("row", "col"),),
        out_specs=P("row", "col"),
        check_vma=False,
    )
```

```python
import jax
import jax.numpy as jnp
from jax import lax
from jax.sharding import PartitionSpec as P

NB = 64
HIGH = lax.Precision.HIGHEST


def both_axes(x, pairs):
    return lax.ppermute(x, ("row", "col"), pairs)


def mm(a, b):
    return jnp.dot(a, b, precision=HIGH, preferred_element_type=jnp.float32)


def gather_corner(stored, swapped, p, q, ncols):
    own = stored[:NB, :NB]
    got = swapped[:NB]
    d00, d01, d10, d11 = 0, 1, ncols, ncols + 1
    from_a = both_axes(own, [(d11, d00), (d00, d10)])
    from_b = both_axes(own, [(d11, d01), (d00, d11)])
    sent = jnp.where(q == 0, from_a, from_b)
    t = jnp.where(q == 0, got, own)
    u = jnp.where(q == 0, own, got)
    a00 = jnp.where(p == 0, u, sent)
    a10 = jnp.where(p == 0, t.T, u)
    a11 = jnp.where(p == 0, sent, t)
    return jnp.concatenate([a00, a10, a11], axis=0)


def spread_round(value, holders, offsets, ncols):
    grown = set(holders)
    total = value
    for dr, dc in offsets:
        pairs = [(r * ncols + c, (r + dr) * ncols + c + dc) for r, c in sorted(holders)]
        total = total + both_axes(value, pairs)
        grown.update((r + dr, c + dc) for r, c in holders)
    return total, grown


def interleave(a, b, count):
    blocks = jnp.stack([a.reshape(count, NB, NB), b.reshape(count, NB, NB)], axis=1)
    return blocks.reshape(2 * count * NB, NB)


def lower_inverse(factor):
    eye = jnp.eye(factor.shape[0], dtype=jnp.float32)
    return jax.scipy.linalg.solve_triangular(factor, eye, lower=True)


def per_device(stored):
    nrows = lax.axis_size("row")
    ncols = lax.axis_size("col")
    assert nrows == 2 * ncols and ncols == 16
    half = nrows // 2
    p = lax.axis_index("row")
    q = lax.axis_index("col")
    row_count = stored.shape[0] // NB
    col_count = stored.shape[1] // NB
    assert col_count == 2 * row_count
    rows_len = row_count * NB

    mine = stored[:, :NB]
    swapped = lax.ppermute(mine, "col", [(0, 1), (1, 0)])
    panel = jnp.concatenate(
        [jnp.where(q == 0, mine, swapped), jnp.where(q == 0, swapped, mine)], axis=0
    )
    panel = jnp.where(q < 2, panel, 0.0)
    corner = jnp.where((p < 2) & (q < 2), gather_corner(stored, swapped, p, q, ncols), 0.0)

    holders_col = [0, 1]
    holders_k = {(0, 0), (0, 1), (1, 0), (1, 1)}
    corner_offsets = [
        [(a * 16 + b * 8, c * 8) for a in (0, 1) for b in (0, 1) for c in (0, 1)][1:],
        [(4, 0), (0, 4), (4, 4)],
        [(2, 0), (0, 2), (2, 2)],
    ]
    for step, offsets in zip((8, 4, 2), corner_offsets):
        panel = panel + lax.ppermute(panel, "col", [(c, c + step) for c in holders_col])
        holders_col = holders_col + [c + step for c in holders_col]
        corner, holders_k = spread_round(corner, holders_k, offsets, ncols)
        if step == 4:
            corner, panel = lax.optimization_barrier((corner, panel))
            early_panel, early_cols = panel, list(holders_col)
    corner, panel_held = lax.optimization_barrier((corner, panel))

    width = len(early_cols)
    groups = nrows // width
    arrivals = []
    for k in range(groups):
        other = (k + groups // 2) % groups
        pairs = []
        for r in range(k * width, (k + 1) * width):
            for c in range(ncols):
                pairs.append((c * ncols + early_cols[r % width], r * ncols + c))
        for r in range(other * width, (other + 1) * width):
            for c in range(ncols):
                pairs.append(((c + half) * ncols + early_cols[r % width], r * ncols + c))
        arrivals.append(both_axes(early_panel, pairs))
    group = p // width
    near = arrivals[0]
    far = arrivals[groups // 2]
    for k in range(groups):
        near = jnp.where(group == k, arrivals[k], near)
        far = jnp.where(group == (k + groups // 2) % groups, arrivals[k], far)

    a00 = corner[:NB]
    a10 = corner[NB : 2 * NB]
    a11 = corner[2 * NB :]
    lead_block = jnp.concatenate(
        [jnp.concatenate([a00, a10.T], axis=1), jnp.concatenate([a10, a11], axis=1)], axis=0
    )
    factor = jnp.linalg.cholesky(lead_block)
    inv_t = lower_inverse(factor).T
    c0 = factor[:NB, :NB]
    c1 = factor[NB:, NB:]
    w_rows = mm(jnp.concatenate([panel_held[:rows_len], panel_held[rows_len:]], axis=1), inv_t)
    x_rows = w_rows[:, :NB]
    y_rows = w_rows[:, NB:]
    v = mm(w_rows, inv_t.T)
    zero_block = jnp.zeros((NB, NB), jnp.float32)

    col0 = interleave(near[:rows_len], far[:rows_len], row_count)
    col1 = interleave(near[rows_len:], far[rows_len:], row_count)
    cols = jnp.concatenate([col0, col1], axis=1)
    update = mm(v, cols.T)

    row_ids = jnp.arange(row_count * NB, dtype=jnp.int32) // NB * nrows + p
    col_ids = jnp.arange(col_count * NB, dtype=jnp.int32) // NB * ncols + q
    keep = (col_ids[None, :] >= 2) & (row_ids[:, None] >= col_ids[None, :])
    result = jnp.where(keep, stored - update, 0.0)

    lead0 = jnp.concatenate([jnp.where(p == 0, c0, x_rows[:NB]), x_rows[NB:]], axis=0)
    lead1_top = jnp.where(p == 0, zero_block, jnp.where(p == 1, c1, y_rows[:NB]))
    lead1 = jnp.concatenate([lead1_top, y_rows[NB:]], axis=0)
    lead = jnp.where(q == 0, lead0, lead1)
    head = jnp.where(q < 2, lead, result[:, :NB])
    return jnp.concatenate([head, result[:, NB:]], axis=1)


def solution(mesh):
    return jax.shard_map(
        per_device,
        mesh=mesh,
        in_specs=(P("row", "col"),),
        out_specs=P("row", "col"),
        check_vma=False,
    )
```

```python
import jax
import jax.numpy as jnp
from jax import lax
from jax.sharding import PartitionSpec as P

NB = 64
HIGH = lax.Precision.HIGHEST


def both_axes(x, pairs):
    return lax.ppermute(x, ("row", "col"), pairs)


def mm(a, b):
    return jnp.dot(a, b, precision=HIGH, preferred_element_type=jnp.float32)


def gather_corner(stored, swapped, p, q, ncols):
    own = stored[:NB, :NB]
    got = swapped[:NB]
    d00, d01, d10, d11 = 0, 1, ncols, ncols + 1
    from_a = both_axes(own, [(d11, d00), (d00, d10)])
    from_b = both_axes(own, [(d11, d01), (d00, d11)])
    sent = jnp.where(q == 0, from_a, from_b)
    t = jnp.where(q == 0, got, own)
    u = jnp.where(q == 0, own, got)
    a00 = jnp.where(p == 0, u, sent)
    a10 = jnp.where(p == 0, t.T, u)
    a11 = jnp.where(p == 0, sent, t)
    return jnp.concatenate([a00, a10, a11], axis=0)


def spread_round(value, holders, offsets, ncols):
    grown = set(holders)
    total = value
    for dr, dc in offsets:
        pairs = [(r * ncols + c, (r + dr) * ncols + c + dc) for r, c in sorted(holders)]
        total = total + both_axes(value, pairs)
        grown.update((r + dr, c + dc) for r, c in holders)
    return total, grown


def interleave(a, b, count):
    blocks = jnp.stack([a.reshape(count, NB, NB), b.reshape(count, NB, NB)], axis=1)
    return blocks.reshape(2 * count * NB, NB)


def lower_inverse(factor):
    eye = jnp.eye(factor.shape[0], dtype=jnp.float32)
    return jax.scipy.linalg.solve_triangular(factor, eye, lower=True)


def per_device(stored):
    nrows = lax.axis_size("row")
    ncols = lax.axis_size("col")
    assert nrows == 2 * ncols and ncols == 16
    half = nrows // 2
    p = lax.axis_index("row")
    q = lax.axis_index("col")
    row_count = stored.shape[0] // NB
    col_count = stored.shape[1] // NB
    assert col_count == 2 * row_count
    rows_len = row_count * NB

    mine = stored[:, :NB]
    swapped = lax.ppermute(mine, "col", [(0, 1), (1, 0)])
    panel = jnp.concatenate(
        [jnp.where(q == 0, mine, swapped), jnp.where(q == 0, swapped, mine)], axis=0
    )
    panel = jnp.where(q < 2, panel, 0.0)
    corner = jnp.where((p < 2) & (q < 2), gather_corner(stored, swapped, p, q, ncols), 0.0)

    holders_col = [0, 1]
    holders_k = {(0, 0), (0, 1), (1, 0), (1, 1)}
    corner_offsets = [
        [(a * 16 + b * 8, c * 8) for a in (0, 1) for b in (0, 1) for c in (0, 1)][1:],
        [(4, 0), (0, 4), (4, 4)],
        [(2, 0), (0, 2), (2, 2)],
    ]
    for step, offsets in zip((8, 4, 2), corner_offsets):
        assert {c for _, c in holders_k} <= set(holders_col) and (0, step) in offsets
        both = jnp.concatenate([panel, corner], axis=0)
        got = lax.ppermute(both, "col", [(c, c + step) for c in holders_col])
        panel = panel + got[: panel.shape[0]]
        along = got[panel.shape[0] :]
        holders_col = holders_col + [c + step for c in holders_col]
        if step == 2:
            corner, panel, along = lax.optimization_barrier((corner, panel, along))
        moved = {(r, c + step) for r, c in holders_k}
        corner, holders_k = spread_round(corner, holders_k, [o for o in offsets if o != (0, step)], ncols)
        corner = corner + along
        holders_k = holders_k | moved
    corner, panel_held = lax.optimization_barrier((corner, panel))

    lin = lambda r, c: r * ncols + c
    first_pairs = [(lin(c, r), lin(r, c)) for r in range(half) for c in range(ncols)]
    first_pairs += [(lin(c + half, r - half), lin(r, c)) for r in range(half, nrows) for c in range(ncols)]
    second_pairs = [(lin(c, r - half), lin(r, c)) for r in range(half, nrows) for c in range(ncols)]
    second_pairs += [(lin(c + half, r), lin(r, c)) for r in range(half) for c in range(ncols)]
    first = both_axes(panel, first_pairs)
    second = both_axes(panel, second_pairs)

    a00 = corner[:NB]
    a10 = corner[NB : 2 * NB]
    a11 = corner[2 * NB :]
    lead_block = jnp.concatenate(
        [jnp.concatenate([a00, a10.T], axis=1), jnp.concatenate([a10, a11], axis=1)], axis=0
    )
    factor = jnp.linalg.cholesky(lead_block)
    inv_t = lower_inverse(factor).T
    c0 = factor[:NB, :NB]
    c1 = factor[NB:, NB:]
    w_rows = mm(jnp.concatenate([panel_held[:rows_len], panel_held[rows_len:]], axis=1), inv_t)
    x_rows = w_rows[:, :NB]
    y_rows = w_rows[:, NB:]
    v = mm(w_rows, inv_t.T)
    zero_block = jnp.zeros((NB, NB), jnp.float32)

    low = p < half
    near = jnp.where(low, first, second)
    far = jnp.where(low, second, first)
    col0 = interleave(near[:rows_len], far[:rows_len], row_count)
    col1 = interleave(near[rows_len:], far[rows_len:], row_count)
    cols = jnp.concatenate([col0, col1], axis=1)
    update = mm(v, cols.T)

    row_ids = jnp.arange(row_count * NB, dtype=jnp.int32) // NB * nrows + p
    col_ids = jnp.arange(col_count * NB, dtype=jnp.int32) // NB * ncols + q
    keep = (col_ids[None, :] >= 2) & (row_ids[:, None] >= col_ids[None, :])
    result = jnp.where(keep, stored - update, 0.0)

    lead0 = jnp.concatenate([jnp.where(p == 0, c0, x_rows[:NB]), x_rows[NB:]], axis=0)
    lead1_top = jnp.where(p == 0, zero_block, jnp.where(p == 1, c1, y_rows[:NB]))
    lead1 = jnp.concatenate([lead1_top, y_rows[NB:]], axis=0)
    lead = jnp.where(q == 0, lead0, lead1)
    head = jnp.where(q < 2, lead, result[:, :NB])
    return jnp.concatenate([head, result[:, NB:]], axis=1)


def solution(mesh):
    return jax.shard_map(
        per_device,
        mesh=mesh,
        in_specs=(P("row", "col"),),
        out_specs=P("row", "col"),
        check_vma=False,
    )
```

```python
import jax
import jax.numpy as jnp
from jax import lax
from jax.sharding import PartitionSpec as P

NB = 64
HIGH = lax.Precision.HIGHEST


def both_axes(x, pairs):
    return lax.ppermute(x, ("row", "col"), pairs)


def mm(a, b):
    return jnp.dot(a, b, precision=HIGH, preferred_element_type=jnp.float32)


def gather_corner(stored, swapped, p, q, ncols):
    own = stored[:NB, :NB]
    got = swapped[:NB]
    d00, d01, d10, d11 = 0, 1, ncols, ncols + 1
    from_a = both_axes(own, [(d11, d00), (d00, d10)])
    from_b = both_axes(own, [(d11, d01), (d00, d11)])
    sent = jnp.where(q == 0, from_a, from_b)
    t = jnp.where(q == 0, got, own)
    u = jnp.where(q == 0, own, got)
    a00 = jnp.where(p == 0, u, sent)
    a10 = jnp.where(p == 0, t.T, u)
    a11 = jnp.where(p == 0, sent, t)
    return jnp.concatenate([a00, a10, a11], axis=0).reshape(3 * NB // 2, 2 * NB)


def spread_round(value, holders, offsets, ncols):
    grown = set(holders)
    total = value
    for dr, dc in offsets:
        pairs = [(r * ncols + c, (r + dr) * ncols + c + dc) for r, c in sorted(holders)]
        total = total + both_axes(value, pairs)
        grown.update((r + dr, c + dc) for r, c in holders)
    return total, grown


def interleave(a, b, count):
    width = a.shape[1]
    blocks = jnp.stack([a.reshape(count, NB, width), b.reshape(count, NB, width)], axis=1)
    return blocks.reshape(2 * count * NB, width)


def lower_inverse(factor):
    eye = jnp.eye(factor.shape[0], dtype=jnp.float32)
    return jax.scipy.linalg.solve_triangular(factor, eye, lower=True)


def per_device(stored):
    nrows = lax.axis_size("row")
    ncols = lax.axis_size("col")
    assert nrows == 2 * ncols and ncols == 16
    half = nrows // 2
    p = lax.axis_index("row")
    q = lax.axis_index("col")
    row_count = stored.shape[0] // NB
    col_count = stored.shape[1] // NB
    assert col_count == 2 * row_count
    rows_len = row_count * NB

    mine = stored[:, :NB]
    swapped = lax.ppermute(mine, "col", [(0, 1), (1, 0)])
    panel = jnp.concatenate(
        [jnp.where(q == 0, mine, swapped), jnp.where(q == 0, swapped, mine)], axis=1
    )
    panel = jnp.where(q < 2, panel, 0.0)
    corner = jnp.where((p < 2) & (q < 2), gather_corner(stored, swapped, p, q, ncols), 0.0)

    holders_col = [0, 1]
    holders_k = {(0, 0), (0, 1), (1, 0), (1, 1)}
    corner_offsets = [
        [(a * 16 + b * 8, c * 8) for a in (0, 1) for b in (0, 1) for c in (0, 1)][1:],
        [(4, 0), (0, 4), (4, 4)],
        [(2, 0), (0, 2), (2, 2)],
    ]
    for step, offsets in zip((8, 4, 2), corner_offsets):
        panel = panel + lax.ppermute(panel, "col", [(c, c + step) for c in holders_col])
        holders_col = holders_col + [c + step for c in holders_col]
        if step == 2:
            corner, panel = lax.optimization_barrier((corner, panel))
        corner, holders_k = spread_round(corner, holders_k, offsets, ncols)
    corner, panel_held = lax.optimization_barrier((corner, panel))

    lin = lambda r, c: r * ncols + c
    first_pairs = [(lin(c, r), lin(r, c)) for r in range(half) for c in range(ncols)]
    first_pairs += [(lin(c + half, r - half), lin(r, c)) for r in range(half, nrows) for c in range(ncols)]
    second_pairs = [(lin(c, r - half), lin(r, c)) for r in range(half, nrows) for c in range(ncols)]
    second_pairs += [(lin(c + half, r), lin(r, c)) for r in range(half) for c in range(ncols)]
    first = both_axes(panel, first_pairs)
    second = both_axes(panel, second_pairs)

    corner = corner.reshape(3 * NB, NB)
    a00 = corner[:NB]
    a10 = corner[NB : 2 * NB]
    a11 = corner[2 * NB :]
    lead_block = jnp.concatenate(
        [jnp.concatenate([a00, a10.T], axis=1), jnp.concatenate([a10, a11], axis=1)], axis=0
    )
    factor = jnp.linalg.cholesky(lead_block)
    inv_t = lower_inverse(factor).T
    c0 = factor[:NB, :NB]
    c1 = factor[NB:, NB:]
    w_rows = mm(panel_held, inv_t)
    x_rows = w_rows[:, :NB]
    y_rows = w_rows[:, NB:]
    v = mm(w_rows, inv_t.T)
    zero_block = jnp.zeros((NB, NB), jnp.float32)

    low = p < half
    near = jnp.where(low, first, second)
    far = jnp.where(low, second, first)
    cols = interleave(near, far, row_count)
    update = mm(v, cols.T)

    row_ids = jnp.arange(row_count * NB, dtype=jnp.int32) // NB * nrows + p
    col_ids = jnp.arange(col_count * NB, dtype=jnp.int32) // NB * ncols + q
    keep = (col_ids[None, :] >= 2) & (row_ids[:, None] >= col_ids[None, :])
    result = jnp.where(keep, stored - update, 0.0)

    lead0 = jnp.concatenate([jnp.where(p == 0, c0, x_rows[:NB]), x_rows[NB:]], axis=0)
    lead1_top = jnp.where(p == 0, zero_block, jnp.where(p == 1, c1, y_rows[:NB]))
    lead1 = jnp.concatenate([lead1_top, y_rows[NB:]], axis=0)
    lead = jnp.where(q == 0, lead0, lead1)
    head = jnp.where(q < 2, lead, result[:, :NB])
    return jnp.concatenate([head, result[:, NB:]], axis=1)


def solution(mesh):
    return jax.shard_map(
        per_device,
        mesh=mesh,
        in_specs=(P("row", "col"),),
        out_specs=P("row", "col"),
        check_vma=False,
    )
```

```python
import jax
import jax.numpy as jnp
from jax import lax
from jax.sharding import PartitionSpec as P

NB = 64
HIGH = lax.Precision.HIGHEST


def both_axes(x, pairs):
    return lax.ppermute(x, ("row", "col"), pairs)


def mm(a, b):
    return jnp.dot(a, b, precision=HIGH, preferred_element_type=jnp.float32)


def gather_corner(stored, swapped, p, q, ncols):
    own = stored[:NB, :NB]
    got = swapped[:NB]
    d00, d01, d10, d11 = 0, 1, ncols, ncols + 1
    from_a = both_axes(own, [(d11, d00), (d00, d10)])
    from_b = both_axes(own, [(d11, d01), (d00, d11)])
    sent = jnp.where(q == 0, from_a, from_b)
    t = jnp.where(q == 0, got, own)
    u = jnp.where(q == 0, own, got)
    a00 = jnp.where(p == 0, u, sent)
    a10 = jnp.where(p == 0, t.T, u)
    a11 = jnp.where(p == 0, sent, t)
    return jnp.concatenate([a00, a10, a11], axis=0).reshape(3 * NB // 2, 2 * NB)


def spread_round(value, holders, offsets, ncols):
    grown = set(holders)
    total = value
    for dr, dc in offsets:
        pairs = [(r * ncols + c, (r + dr) * ncols + c + dc) for r, c in sorted(holders)]
        total = total + both_axes(value, pairs)
        grown.update((r + dr, c + dc) for r, c in holders)
    return total, grown


def interleave(a, b, count):
    width = a.shape[1]
    blocks = jnp.stack([a.reshape(count, NB, width), b.reshape(count, NB, width)], axis=1)
    return blocks.reshape(2 * count * NB, width)


def lower_inverse(factor):
    eye = jnp.eye(factor.shape[0], dtype=jnp.float32)
    return jax.scipy.linalg.solve_triangular(factor, eye, lower=True)


def per_device(stored):
    nrows = lax.axis_size("row")
    ncols = lax.axis_size("col")
    assert nrows == 2 * ncols and ncols == 16
    half = nrows // 2
    p = lax.axis_index("row")
    q = lax.axis_index("col")
    row_count = stored.shape[0] // NB
    col_count = stored.shape[1] // NB
    assert col_count == 2 * row_count
    rows_len = row_count * NB

    mine = stored[:, :NB]
    swapped = lax.ppermute(mine, "col", [(0, 1), (1, 0)])
    panel = jnp.concatenate(
        [jnp.where(q == 0, mine, swapped), jnp.where(q == 0, swapped, mine)], axis=1
    )
    panel = jnp.where(q < 2, panel, 0.0)
    corner = jnp.where((p < 2) & (q < 2), gather_corner(stored, swapped, p, q, ncols), 0.0)

    holders_col = [0, 1]
    holders_k = {(0, 0), (0, 1), (1, 0), (1, 1)}
    corner_offsets = [
        [(a * 16 + b * 8, c * 8) for a in (0, 1) for b in (0, 1) for c in (0, 1)][1:],
        [(4, 0), (0, 4), (4, 4)],
        [(2, 0), (0, 2), (2, 2)],
    ]
    panel_rounds = [
        [[(0, 8), (1, 9)], [(0, 4), (1, 5)]],
        [[(0, 2), (1, 3), (4, 6), (5, 7), (8, 10), (9, 11)], [(8, 12), (9, 13), (4, 14), (5, 15)]],
    ]
    for pairs_list, offsets in zip(panel_rounds, corner_offsets[:2]):
        sent = panel
        for pairs in pairs_list:
            panel = panel + lax.ppermute(sent, "col", pairs)
            holders_col = holders_col + [dst for _, dst in pairs]
        corner, holders_k = spread_round(corner, holders_k, offsets, ncols)
    assert sorted(holders_col) == list(range(ncols))
    corner, panel = lax.optimization_barrier((corner, panel))
    corner, holders_k = spread_round(corner, holders_k, corner_offsets[2], ncols)
    assert len(holders_k) == nrows * ncols
    corner, panel_held = lax.optimization_barrier((corner, panel))

    lin = lambda r, c: r * ncols + c
    first_pairs = [(lin(c, r), lin(r, c)) for r in range(half) for c in range(ncols)]
    first_pairs += [(lin(c + half, r - half), lin(r, c)) for r in range(half, nrows) for c in range(ncols)]
    second_pairs = [(lin(c, r - half), lin(r, c)) for r in range(half, nrows) for c in range(ncols)]
    second_pairs += [(lin(c + half, r), lin(r, c)) for r in range(half) for c in range(ncols)]
    first = both_axes(panel, first_pairs)
    second = both_axes(panel, second_pairs)

    corner = corner.reshape(3 * NB, NB)
    a00 = corner[:NB]
    a10 = corner[NB : 2 * NB]
    a11 = corner[2 * NB :]
    lead_block = jnp.concatenate(
        [jnp.concatenate([a00, a10.T], axis=1), jnp.concatenate([a10, a11], axis=1)], axis=0
    )
    factor = jnp.linalg.cholesky(lead_block)
    inv_t = lower_inverse(factor).T
    c0 = factor[:NB, :NB]
    c1 = factor[NB:, NB:]
    w_rows = mm(panel_held, inv_t)
    x_rows = w_rows[:, :NB]
    y_rows = w_rows[:, NB:]
    v = mm(w_rows, inv_t.T)
    zero_block = jnp.zeros((NB, NB), jnp.float32)

    low = p < half
    near = jnp.where(low, first, second)
    far = jnp.where(low, second, first)
    cols = interleave(near, far, row_count)
    update = mm(v, cols.T)

    row_ids = jnp.arange(row_count * NB, dtype=jnp.int32) // NB * nrows + p
    col_ids = jnp.arange(col_count * NB, dtype=jnp.int32) // NB * ncols + q
    keep = (col_ids[None, :] >= 2) & (row_ids[:, None] >= col_ids[None, :])
    result = jnp.where(keep, stored - update, 0.0)

    lead0 = jnp.concatenate([jnp.where(p == 0, c0, x_rows[:NB]), x_rows[NB:]], axis=0)
    lead1_top = jnp.where(p == 0, zero_block, jnp.where(p == 1, c1, y_rows[:NB]))
    lead1 = jnp.concatenate([lead1_top, y_rows[NB:]], axis=0)
    lead = jnp.where(q == 0, lead0, lead1)
    head = jnp.where(q < 2, lead, result[:, :NB])
    return jnp.concatenate([head, result[:, NB:]], axis=1)


def solution(mesh):
    return jax.shard_map(
        per_device,
        mesh=mesh,
        in_specs=(P("row", "col"),),
        out_specs=P("row", "col"),
        check_vma=False,
    )
```

```python
import jax
import jax.numpy as jnp
from jax import lax
from jax.sharding import PartitionSpec as P

NB = 64
HIGH = lax.Precision.HIGHEST


def both_axes(x, pairs):
    return lax.ppermute(x, ("row", "col"), pairs)


def mm(a, b):
    return jnp.dot(a, b, precision=HIGH, preferred_element_type=jnp.float32)


def gather_corner(stored, swapped, p, q, ncols):
    own = stored[:NB, :NB]
    got = swapped[:NB]
    d00, d01, d10, d11 = 0, 1, ncols, ncols + 1
    from_a = both_axes(own, [(d11, d00), (d00, d10)])
    from_b = both_axes(own, [(d11, d01), (d00, d11)])
    sent = jnp.where(q == 0, from_a, from_b)
    t = jnp.where(q == 0, got, own)
    u = jnp.where(q == 0, own, got)
    a00 = jnp.where(p == 0, u, sent)
    a10 = jnp.where(p == 0, t.T, u)
    a11 = jnp.where(p == 0, sent, t)
    return jnp.concatenate([a00, a10, a11], axis=0).reshape(3 * NB // 2, 2 * NB)


def spread_round(value, holders, offsets, ncols):
    grown = set(holders)
    total = value
    for dr, dc in offsets:
        pairs = [(r * ncols + c, (r + dr) * ncols + c + dc) for r, c in sorted(holders)]
        total = total + both_axes(value, pairs)
        grown.update((r + dr, c + dc) for r, c in holders)
    return total, grown


def interleave(a, b, count):
    width = a.shape[1]
    blocks = jnp.stack([a.reshape(count, NB, width), b.reshape(count, NB, width)], axis=1)
    return blocks.reshape(2 * count * NB, width)


def lower_inverse(factor):
    eye = jnp.eye(factor.shape[0], dtype=jnp.float32)
    return jax.scipy.linalg.solve_triangular(factor, eye, lower=True)


def per_device(stored):
    nrows = lax.axis_size("row")
    ncols = lax.axis_size("col")
    assert nrows == 2 * ncols and ncols == 16
    half = nrows // 2
    p = lax.axis_index("row")
    q = lax.axis_index("col")
    row_count = stored.shape[0] // NB
    col_count = stored.shape[1] // NB
    assert col_count == 2 * row_count
    rows_len = row_count * NB

    mine = stored[:, :NB]
    swapped = lax.ppermute(mine, "col", [(0, 1), (1, 0)])
    panel = jnp.concatenate(
        [jnp.where(q == 0, mine, swapped), jnp.where(q == 0, swapped, mine)], axis=1
    )
    panel = jnp.where(q < 2, panel, 0.0)
    corner = jnp.where((p < 2) & (q < 2), gather_corner(stored, swapped, p, q, ncols), 0.0)

    holders_col = [0, 1]
    holders_k = {(0, 0), (0, 1), (1, 0), (1, 1)}
    corner_offsets = [
        [(a * 16 + b * 8, c * 8) for a in (0, 1) for b in (0, 1) for c in (0, 1)][1:],
        [(4, 0), (0, 4), (4, 4)],
        [(2, 0), (0, 2), (2, 2)],
    ]
    panel_rounds = [
        [[(0, 8), (1, 9)], [(0, 12), (1, 13)]],
        [[(0, 2), (1, 3), (8, 10), (9, 11), (12, 14), (13, 15)], [(8, 6), (9, 7), (0, 4), (1, 5)]],
    ]
    for pairs_list, offsets in zip(panel_rounds, corner_offsets[:2]):
        sent = panel
        for pairs in pairs_list:
            panel = panel + lax.ppermute(sent, "col", pairs)
            holders_col = holders_col + [dst for _, dst in pairs]
        corner, holders_k = spread_round(corner, holders_k, offsets, ncols)
    assert sorted(holders_col) == list(range(ncols))
    corner, panel = lax.optimization_barrier((corner, panel))
    corner, holders_k = spread_round(corner, holders_k, corner_offsets[2], ncols)
    assert len(holders_k) == nrows * ncols
    corner, panel_held = lax.optimization_barrier((corner, panel))

    lin = lambda r, c: r * ncols + c
    first_pairs = [(lin(c, r), lin(r, c)) for r in range(half) for c in range(ncols)]
    first_pairs += [(lin(c + half, r - half), lin(r, c)) for r in range(half, nrows) for c in range(ncols)]
    second_pairs = [(lin(c, r - half), lin(r, c)) for r in range(half, nrows) for c in range(ncols)]
    second_pairs += [(lin(c + half, r), lin(r, c)) for r in range(half) for c in range(ncols)]
    first = both_axes(panel, first_pairs)
    second = both_axes(panel, second_pairs)

    corner = corner.reshape(3 * NB, NB)
    a00 = corner[:NB]
    a10 = corner[NB : 2 * NB]
    a11 = corner[2 * NB :]
    lead_block = jnp.concatenate(
        [jnp.concatenate([a00, a10.T], axis=1), jnp.concatenate([a10, a11], axis=1)], axis=0
    )
    factor = jnp.linalg.cholesky(lead_block)
    inv_t = lower_inverse(factor).T
    c0 = factor[:NB, :NB]
    c1 = factor[NB:, NB:]
    w_rows = mm(panel_held, inv_t)
    x_rows = w_rows[:, :NB]
    y_rows = w_rows[:, NB:]
    v = mm(w_rows, inv_t.T)
    zero_block = jnp.zeros((NB, NB), jnp.float32)

    low = p < half
    near = jnp.where(low, first, second)
    far = jnp.where(low, second, first)
    cols = interleave(near, far, row_count)
    update = mm(v, cols.T)

    row_ids = jnp.arange(row_count * NB, dtype=jnp.int32) // NB * nrows + p
    col_ids = jnp.arange(col_count * NB, dtype=jnp.int32) // NB * ncols + q
    keep = (col_ids[None, :] >= 2) & (row_ids[:, None] >= col_ids[None, :])
    result = jnp.where(keep, stored - update, 0.0)

    lead0 = jnp.concatenate([jnp.where(p == 0, c0, x_rows[:NB]), x_rows[NB:]], axis=0)
    lead1_top = jnp.where(p == 0, zero_block, jnp.where(p == 1, c1, y_rows[:NB]))
    lead1 = jnp.concatenate([lead1_top, y_rows[NB:]], axis=0)
    lead = jnp.where(q == 0, lead0, lead1)
    head = jnp.where(q < 2, lead, result[:, :NB])
    return jnp.concatenate([head, result[:, NB:]], axis=1)


def solution(mesh):
    return jax.shard_map(
        per_device,
        mesh=mesh,
        in_specs=(P("row", "col"),),
        out_specs=P("row", "col"),
        check_vma=False,
    )
```

```python
import jax
import jax.numpy as jnp
from jax import lax
from jax.sharding import PartitionSpec as P

NB = 64
HIGH = lax.Precision.HIGHEST


def both_axes(x, pairs):
    return lax.ppermute(x, ("row", "col"), pairs)


def mm(a, b):
    return jnp.dot(a, b, precision=HIGH, preferred_element_type=jnp.float32)


def gather_corner(stored, swapped, p, q, ncols):
    own = stored[:NB, :NB]
    got = swapped[:NB]
    d00, d01, d10, d11 = 0, 1, ncols, ncols + 1
    from_a = both_axes(own, [(d11, d00), (d00, d10)])
    from_b = both_axes(own, [(d11, d01), (d00, d11)])
    sent = jnp.where(q == 0, from_a, from_b)
    t = jnp.where(q == 0, got, own)
    u = jnp.where(q == 0, own, got)
    a00 = jnp.where(p == 0, u, sent)
    a10 = jnp.where(p == 0, t.T, u)
    a11 = jnp.where(p == 0, sent, t)
    return jnp.concatenate([a00, a10, a11], axis=0).reshape(3 * NB // 2, 2 * NB)


def spread_round(value, holders, offsets, ncols):
    grown = set(holders)
    total = value
    for dr, dc in offsets:
        pairs = [(r * ncols + c, (r + dr) * ncols + c + dc) for r, c in sorted(holders)]
        total = total + both_axes(value, pairs)
        grown.update((r + dr, c + dc) for r, c in holders)
    return total, grown


def interleave(a, b, count):
    width = a.shape[1]
    blocks = jnp.stack([a.reshape(count, NB, width), b.reshape(count, NB, width)], axis=1)
    return blocks.reshape(2 * count * NB, width)


def lower_inverse(factor):
    eye = jnp.eye(factor.shape[0], dtype=jnp.float32)
    return jax.scipy.linalg.solve_triangular(factor, eye, lower=True)


def per_device(stored):
    nrows = lax.axis_size("row")
    ncols = lax.axis_size("col")
    assert nrows == 2 * ncols and ncols == 16
    half = nrows // 2
    p = lax.axis_index("row")
    q = lax.axis_index("col")
    row_count = stored.shape[0] // NB
    col_count = stored.shape[1] // NB
    assert col_count == 2 * row_count
    rows_len = row_count * NB

    mine = stored[:, :NB]
    swapped = lax.ppermute(mine, "col", [(0, 1), (1, 0)])
    panel = jnp.concatenate(
        [jnp.where(q == 0, mine, swapped), jnp.where(q == 0, swapped, mine)], axis=1
    )
    panel = jnp.where(q < 2, panel, 0.0)
    corner = jnp.where((p < 2) & (q < 2), gather_corner(stored, swapped, p, q, ncols), 0.0)

    holders_col = [0, 1]
    holders_k = {(0, 0), (0, 1), (1, 0), (1, 1)}
    corner_offsets = [
        [(a * 16 + b * 8, c * 8) for a in (0, 1) for b in (0, 1) for c in (0, 1)][1:],
        [(4, 0), (0, 4), (4, 4)],
        [(2, 0), (0, 2), (2, 2)],
    ]
    panel_rounds = [
        [[(0, 8), (1, 9)], [(0, 4), (1, 5)]],
        [[(0, 2), (1, 3), (4, 6), (5, 7), (8, 10), (9, 11)], [(8, 12), (9, 13), (4, 14), (5, 15)]],
    ]
    for pairs_list, offsets in zip(panel_rounds, corner_offsets[:2]):
        sent = panel
        for pairs in pairs_list:
            panel = panel + lax.ppermute(sent, "col", pairs)
            holders_col = holders_col + [dst for _, dst in pairs]
        corner, holders_k = spread_round(corner, holders_k, offsets, ncols)
    assert sorted(holders_col) == list(range(ncols))
    corner, panel = lax.optimization_barrier((corner, panel))
    corner, holders_k = spread_round(corner, holders_k, corner_offsets[2], ncols)
    assert len(holders_k) == nrows * ncols
    corner, panel_held = lax.optimization_barrier((corner, panel))

    lin = lambda r, c: r * ncols + c
    first_pairs = [(lin(c, r), lin(r, c)) for r in range(half) for c in range(ncols)]
    first_pairs += [(lin(c + half, r - half), lin(r, c)) for r in range(half, nrows) for c in range(ncols)]
    second_pairs = [(lin(c, r - half), lin(r, c)) for r in range(half, nrows) for c in range(ncols)]
    second_pairs += [(lin(c + half, r), lin(r, c)) for r in range(half) for c in range(ncols)]
    first = both_axes(panel, first_pairs)
    second = both_axes(panel, second_pairs)

    corner = corner.reshape(3 * NB, NB)
    a00 = corner[:NB]
    a10 = corner[NB : 2 * NB]
    a11 = corner[2 * NB :]
    lead_block = jnp.concatenate(
        [jnp.concatenate([a00, a10.T], axis=1), jnp.concatenate([a10, a11], axis=1)], axis=0
    )
    factor = jnp.linalg.cholesky(lead_block)
    inv_t = lower_inverse(factor).T
    c0 = factor[:NB, :NB]
    c1 = factor[NB:, NB:]
    w_rows = mm(panel_held, inv_t)
    x_rows = w_rows[:, :NB]
    y_rows = w_rows[:, NB:]
    v = mm(w_rows, inv_t.T)
    zero_block = jnp.zeros((NB, NB), jnp.float32)

    low = p < half
    near = jnp.where(low, first, second)
    far = jnp.where(low, second, first)
    cols = interleave(near, far, row_count)
    update = mm(v, cols.T)

    row_ids = jnp.arange(row_count * NB, dtype=jnp.int32) // NB * nrows + p
    col_ids = jnp.arange(col_count * NB, dtype=jnp.int32) // NB * ncols + q
    keep = (col_ids[None, :] >= 2) & (row_ids[:, None] >= col_ids[None, :])
    result = jnp.where(keep, stored - update, 0.0)

    lead0 = jnp.concatenate([jnp.where(p == 0, c0, x_rows[:NB]), x_rows[NB:]], axis=0)
    lead1_top = jnp.where(p == 0, zero_block, jnp.where(p == 1, c1, y_rows[:NB]))
    lead1 = jnp.concatenate([lead1_top, y_rows[NB:]], axis=0)
    lead = jnp.where(q == 0, lead0, lead1)
    head = jnp.where(q < 2, lead, result[:, :NB])
    return lax.dynamic_update_slice(result, head, (0, 0))


def solution(mesh):
    return jax.shard_map(
        per_device,
        mesh=mesh,
        in_specs=(P("row", "col"),),
        out_specs=P("row", "col"),
        check_vma=False,
    )
```

```python
import jax
import jax.numpy as jnp
from jax import lax
from jax.sharding import PartitionSpec as P

NB = 64
HIGH = lax.Precision.HIGHEST


def both_axes(x, pairs):
    return lax.ppermute(x, ("row", "col"), pairs)


def mm(a, b):
    return jnp.dot(a, b, precision=HIGH, preferred_element_type=jnp.float32)


def gather_corner(stored, swapped, p, q, ncols):
    own = stored[:NB, :NB]
    got = swapped[:NB]
    d00, d01, d10, d11 = 0, 1, ncols, ncols + 1
    from_a = both_axes(own, [(d11, d00), (d00, d10)])
    from_b = both_axes(own, [(d11, d01), (d00, d11)])
    sent = jnp.where(q == 0, from_a, from_b)
    t = jnp.where(q == 0, got, own)
    u = jnp.where(q == 0, own, got)
    a00 = jnp.where(p == 0, u, sent)
    a10 = jnp.where(p == 0, t.T, u)
    a11 = jnp.where(p == 0, sent, t)
    return jnp.concatenate([a00, a10, a11], axis=0).reshape(3 * NB // 2, 2 * NB)


def spread_round(value, holders, offsets, ncols):
    grown = set(holders)
    total = value
    for dr, dc in offsets:
        pairs = [(r * ncols + c, (r + dr) * ncols + c + dc) for r, c in sorted(holders)]
        total = total + both_axes(value, pairs)
        grown.update((r + dr, c + dc) for r, c in holders)
    return total, grown


def interleave(a, b, count):
    width = a.shape[1]
    blocks = jnp.stack([a.reshape(count, NB, width), b.reshape(count, NB, width)], axis=1)
    return blocks.reshape(2 * count * NB, width)


def lower_inverse(factor):
    eye = jnp.eye(factor.shape[0], dtype=jnp.float32)
    return jax.scipy.linalg.solve_triangular(factor, eye, lower=True)


def per_device(stored):
    nrows = lax.axis_size("row")
    ncols = lax.axis_size("col")
    assert nrows == 2 * ncols and ncols == 16
    half = nrows // 2
    p = lax.axis_index("row")
    q = lax.axis_index("col")
    row_count = stored.shape[0] // NB
    col_count = stored.shape[1] // NB
    assert col_count == 2 * row_count
    rows_len = row_count * NB

    mine = stored[:, :NB]
    swapped = lax.ppermute(mine, "col", [(0, 1), (1, 0)])
    panel = jnp.concatenate(
        [jnp.where(q == 0, mine, swapped), jnp.where(q == 0, swapped, mine)], axis=1
    )
    panel = jnp.where(q < 2, panel, 0.0)
    corner = jnp.where((p < 2) & (q < 2), gather_corner(stored, swapped, p, q, ncols), 0.0)

    holders_col = [0, 1]
    holders_k = {(0, 0), (0, 1), (1, 0), (1, 1)}
    corner_offsets = [
        [(a * 16 + b * 8, c * 8) for a in (0, 1) for b in (0, 1) for c in (0, 1)][1:],
        [(a * 4 + b * 2, c * 4) for a in (0, 1) for b in (0, 1) for c in (0, 1)][1:],
        [(0, 2)],
    ]
    panel_rounds = [
        [[(0, 8), (1, 9)], [(0, 4), (1, 5)]],
        [[(0, 2), (1, 3), (4, 6), (5, 7), (8, 10), (9, 11)], [(8, 12), (9, 13), (4, 14), (5, 15)]],
    ]
    for pairs_list, offsets in zip(panel_rounds, corner_offsets[:2]):
        sent = panel
        for pairs in pairs_list:
            panel = panel + lax.ppermute(sent, "col", pairs)
            holders_col = holders_col + [dst for _, dst in pairs]
        corner, holders_k = spread_round(corner, holders_k, offsets, ncols)
    assert sorted(holders_col) == list(range(ncols))
    corner, panel = lax.optimization_barrier((corner, panel))
    corner, holders_k = spread_round(corner, holders_k, corner_offsets[2], ncols)
    assert len(holders_k) == nrows * ncols
    corner, panel_held = lax.optimization_barrier((corner, panel))

    lin = lambda r, c: r * ncols + c
    first_pairs = [(lin(c, r), lin(r, c)) for r in range(half) for c in range(ncols)]
    first_pairs += [(lin(c + half, r - half), lin(r, c)) for r in range(half, nrows) for c in range(ncols)]
    second_pairs = [(lin(c, r - half), lin(r, c)) for r in range(half, nrows) for c in range(ncols)]
    second_pairs += [(lin(c + half, r), lin(r, c)) for r in range(half) for c in range(ncols)]
    first = both_axes(panel, first_pairs)
    second = both_axes(panel, second_pairs)

    corner = corner.reshape(3 * NB, NB)
    a00 = corner[:NB]
    a10 = corner[NB : 2 * NB]
    a11 = corner[2 * NB :]
    lead_block = jnp.concatenate(
        [jnp.concatenate([a00, a10.T], axis=1), jnp.concatenate([a10, a11], axis=1)], axis=0
    )
    factor = jnp.linalg.cholesky(lead_block)
    inv_t = lower_inverse(factor).T
    c0 = factor[:NB, :NB]
    c1 = factor[NB:, NB:]
    w_rows = mm(panel_held, inv_t)
    x_rows = w_rows[:, :NB]
    y_rows = w_rows[:, NB:]
    v = mm(w_rows, inv_t.T)
    zero_block = jnp.zeros((NB, NB), jnp.float32)

    low = p < half
    near = jnp.where(low, first, second)
    far = jnp.where(low, second, first)
    cols = interleave(near, far, row_count)
    update = mm(v, cols.T)

    row_ids = jnp.arange(row_count * NB, dtype=jnp.int32) // NB * nrows + p
    col_ids = jnp.arange(col_count * NB, dtype=jnp.int32) // NB * ncols + q
    keep = (col_ids[None, :] >= 2) & (row_ids[:, None] >= col_ids[None, :])
    result = jnp.where(keep, stored - update, 0.0)

    lead0 = jnp.concatenate([jnp.where(p == 0, c0, x_rows[:NB]), x_rows[NB:]], axis=0)
    lead1_top = jnp.where(p == 0, zero_block, jnp.where(p == 1, c1, y_rows[:NB]))
    lead1 = jnp.concatenate([lead1_top, y_rows[NB:]], axis=0)
    lead = jnp.where(q == 0, lead0, lead1)
    head = jnp.where(q < 2, lead, result[:, :NB])
    return jnp.concatenate([head, result[:, NB:]], axis=1)


def solution(mesh):
    return jax.shard_map(
        per_device,
        mesh=mesh,
        in_specs=(P("row", "col"),),
        out_specs=P("row", "col"),
        check_vma=False,
    )
```

```python
import jax
import jax.numpy as jnp
from jax import lax
from jax.sharding import PartitionSpec as P

NB = 64
HIGH = lax.Precision.HIGHEST


def both_axes(x, pairs):
    return lax.ppermute(x, ("row", "col"), pairs)


def mm(a, b):
    return jnp.dot(a, b, precision=HIGH, preferred_element_type=jnp.float32)


def gather_corner(stored, swapped, p, q, ncols):
    own = stored[:NB, :NB]
    got = swapped[:NB]
    d00, d01, d10, d11 = 0, 1, ncols, ncols + 1
    from_a = both_axes(own, [(d11, d00), (d00, d10)])
    from_b = both_axes(own, [(d11, d01), (d00, d11)])
    sent = jnp.where(q == 0, from_a, from_b)
    t = jnp.where(q == 0, got, own)
    u = jnp.where(q == 0, own, got)
    a00 = jnp.where(p == 0, u, sent)
    a10 = jnp.where(p == 0, t.T, u)
    a11 = jnp.where(p == 0, sent, t)
    return jnp.concatenate([a00, a10, a11], axis=0).reshape(3 * NB // 2, 2 * NB)


def spread_round(value, holders, offsets, ncols):
    grown = set(holders)
    total = value
    for dr, dc in offsets:
        pairs = [(r * ncols + c, (r + dr) * ncols + c + dc) for r, c in sorted(holders)]
        total = total + both_axes(value, pairs)
        grown.update((r + dr, c + dc) for r, c in holders)
    return total, grown


def interleave(a, b, count):
    width = a.shape[1]
    blocks = jnp.stack([a.reshape(count, NB, width), b.reshape(count, NB, width)], axis=1)
    return blocks.reshape(2 * count * NB, width)


def lower_inverse(factor):
    eye = jnp.eye(factor.shape[0], dtype=jnp.float32)
    return jax.scipy.linalg.solve_triangular(factor, eye, lower=True)


def per_device(stored):
    nrows = lax.axis_size("row")
    ncols = lax.axis_size("col")
    assert nrows == 2 * ncols and ncols == 16
    half = nrows // 2
    p = lax.axis_index("row")
    q = lax.axis_index("col")
    row_count = stored.shape[0] // NB
    col_count = stored.shape[1] // NB
    assert col_count == 2 * row_count
    rows_len = row_count * NB

    mine = stored[:, :NB]
    swapped = lax.ppermute(mine, "col", [(0, 1), (1, 0)])
    panel = jnp.concatenate(
        [jnp.where(q == 0, mine, swapped), jnp.where(q == 0, swapped, mine)], axis=1
    )
    panel = jnp.where(q < 2, panel, 0.0)
    corner = jnp.where((p < 2) & (q < 2), gather_corner(stored, swapped, p, q, ncols), 0.0)

    holders_col = [0, 1]
    holders_k = {(0, 0), (0, 1), (1, 0), (1, 1)}
    corner_offsets = [
        [(a * 16 + b * 8, c * 8) for a in (0, 1) for b in (0, 1) for c in (0, 1)][1:],
        [(4, 0), (0, 4), (4, 4)],
        [(2, 0), (0, 2), (2, 2)],
    ]
    panel_rounds = [
        [[(0, 8), (1, 9)], [(0, 4), (1, 5)]],
        [[(0, 2), (1, 3), (4, 6), (5, 7), (8, 10), (9, 11)], [(8, 12), (9, 13), (4, 14), (5, 15)]],
    ]
    for pairs_list, offsets in zip(panel_rounds, corner_offsets[:2]):
        sent = panel
        for pairs in pairs_list:
            panel = panel + lax.ppermute(sent, "col", pairs)
            holders_col = holders_col + [dst for _, dst in pairs]
        corner, holders_k = spread_round(corner, holders_k, offsets, ncols)
    assert sorted(holders_col) == list(range(ncols))
    corner, panel = lax.optimization_barrier((corner, panel))
    corner, holders_k = spread_round(corner, holders_k, corner_offsets[2], ncols)
    assert len(holders_k) == nrows * ncols
    corner, panel_held = lax.optimization_barrier((corner, panel))

    lin = lambda r, c: r * ncols + c
    first_pairs = [(lin(c, r), lin(r, c)) for r in range(half) for c in range(ncols)]
    first_pairs += [(lin(c + half, r - half), lin(r, c)) for r in range(half, nrows) for c in range(ncols)]
    second_pairs = [(lin(c, r - half), lin(r, c)) for r in range(half, nrows) for c in range(ncols)]
    second_pairs += [(lin(c + half, r), lin(r, c)) for r in range(half) for c in range(ncols)]
    first = both_axes(panel, first_pairs)
    second = both_axes(panel, second_pairs)

    corner = corner.reshape(3 * NB, NB)
    a00 = corner[:NB]
    a10 = corner[NB : 2 * NB]
    a11 = corner[2 * NB :]
    lead_block = jnp.concatenate(
        [jnp.concatenate([a00, a10.T], axis=1), jnp.concatenate([a10, a11], axis=1)], axis=0
    )
    factor = jnp.linalg.cholesky(lead_block)
    c0 = factor[:NB, :NB]
    c1 = factor[NB:, NB:]
    eye = jnp.broadcast_to(jnp.eye(NB, dtype=jnp.float32), (2, NB, NB))
    diag_inv = jax.scipy.linalg.solve_triangular(jnp.stack([c0, c1]), eye, lower=True)
    inv0, inv1 = diag_inv[0], diag_inv[1]
    off = -mm(mm(inv1, factor[NB:, :NB]), inv0)
    zero_block = jnp.zeros((NB, NB), jnp.float32)
    inv_lower = jnp.concatenate(
        [jnp.concatenate([inv0, zero_block], axis=1), jnp.concatenate([off, inv1], axis=1)], axis=0
    )
    inv_t = inv_lower.T
    w_rows = mm(panel_held, inv_t)
    x_rows = w_rows[:, :NB]
    y_rows = w_rows[:, NB:]
    v = mm(w_rows, inv_t.T)

    low = p < half
    near = jnp.where(low, first, second)
    far = jnp.where(low, second, first)
    cols = interleave(near, far, row_count)
    update = mm(v, cols.T)

    row_ids = jnp.arange(row_count * NB, dtype=jnp.int32) // NB * nrows + p
    col_ids = jnp.arange(col_count * NB, dtype=jnp.int32) // NB * ncols + q
    keep = (col_ids[None, :] >= 2) & (row_ids[:, None] >= col_ids[None, :])
    result = jnp.where(keep, stored - update, 0.0)

    lead0 = jnp.concatenate([jnp.where(p == 0, c0, x_rows[:NB]), x_rows[NB:]], axis=0)
    lead1_top = jnp.where(p == 0, zero_block, jnp.where(p == 1, c1, y_rows[:NB]))
    lead1 = jnp.concatenate([lead1_top, y_rows[NB:]], axis=0)
    lead = jnp.where(q == 0, lead0, lead1)
    head = jnp.where(q < 2, lead, result[:, :NB])
    return jnp.concatenate([head, result[:, NB:]], axis=1)


def solution(mesh):
    return jax.shard_map(
        per_device,
        mesh=mesh,
        in_specs=(P("row", "col"),),
        out_specs=P("row", "col"),
        check_vma=False,
    )
```

```python
import jax
import jax.numpy as jnp
from jax import lax
from jax.sharding import PartitionSpec as P

NB = 64
HIGH = lax.Precision.HIGHEST


def both_axes(x, pairs):
    return lax.ppermute(x, ("row", "col"), pairs)


def mm(a, b):
    return jnp.dot(a, b, precision=HIGH, preferred_element_type=jnp.float32)


def gather_corner(stored, swapped, p, q, ncols):
    own = stored[:NB, :NB]
    got = swapped[:NB]
    d00, d01, d10, d11 = 0, 1, ncols, ncols + 1
    from_a = both_axes(own, [(d11, d00), (d00, d10)])
    from_b = both_axes(own, [(d11, d01), (d00, d11)])
    sent = jnp.where(q == 0, from_a, from_b)
    t = jnp.where(q == 0, got, own)
    u = jnp.where(q == 0, own, got)
    a00 = jnp.where(p == 0, u, sent)
    a10 = jnp.where(p == 0, t.T, u)
    a11 = jnp.where(p == 0, sent, t)
    return pack_corner(a00, a10, a11)


def pack_corner(a00, a10, a11):
    r = lax.broadcasted_iota(jnp.int32, (NB, NB), 0)
    c = lax.broadcasted_iota(jnp.int32, (NB, NB), 1)
    shared = jnp.where(r >= c, a00, a11)
    diag = jnp.sum(jnp.where(r == c, a11, 0.0), axis=0, keepdims=True)
    last = jnp.concatenate([diag, jnp.zeros((1, NB), jnp.float32)], axis=1)
    return jnp.concatenate([jnp.concatenate([shared, a10], axis=1), last], axis=0)


def unpack_corner(packed):
    r = lax.broadcasted_iota(jnp.int32, (NB, NB), 0)
    c = lax.broadcasted_iota(jnp.int32, (NB, NB), 1)
    shared = packed[:NB, :NB]
    a10 = packed[:NB, NB:]
    diag = packed[NB:, :NB]
    a00 = jnp.where(r >= c, shared, shared.T)
    a11 = jnp.where(r == c, diag, jnp.where(r < c, shared, shared.T))
    return a00, a10, a11


def spread_round(value, holders, offsets, ncols):
    grown = set(holders)
    total = value
    for dr, dc in offsets:
        pairs = [(r * ncols + c, (r + dr) * ncols + c + dc) for r, c in sorted(holders)]
        total = total + both_axes(value, pairs)
        grown.update((r + dr, c + dc) for r, c in holders)
    return total, grown


def interleave(a, b, count):
    width = a.shape[1]
    blocks = jnp.stack([a.reshape(count, NB, width), b.reshape(count, NB, width)], axis=1)
    return blocks.reshape(2 * count * NB, width)


def lower_inverse(factor):
    eye = jnp.eye(factor.shape[0], dtype=jnp.float32)
    return jax.scipy.linalg.solve_triangular(factor, eye, lower=True)


def per_device(stored):
    nrows = lax.axis_size("row")
    ncols = lax.axis_size("col")
    assert nrows == 2 * ncols and ncols == 16
    half = nrows // 2
    p = lax.axis_index("row")
    q = lax.axis_index("col")
    row_count = stored.shape[0] // NB
    col_count = stored.shape[1] // NB
    assert col_count == 2 * row_count
    rows_len = row_count * NB

    mine = stored[:, :NB]
    swapped = lax.ppermute(mine, "col", [(0, 1), (1, 0)])
    panel = jnp.concatenate(
        [jnp.where(q == 0, mine, swapped), jnp.where(q == 0, swapped, mine)], axis=1
    )
    panel = jnp.where(q < 2, panel, 0.0)
    corner = jnp.where((p < 2) & (q < 2), gather_corner(stored, swapped, p, q, ncols), 0.0)

    holders_col = [0, 1]
    holders_k = {(0, 0), (0, 1), (1, 0), (1, 1)}
    corner_offsets = [
        [(a * 16 + b * 8, c * 8) for a in (0, 1) for b in (0, 1) for c in (0, 1)][1:],
        [(4, 0), (0, 4), (4, 4)],
        [(2, 0), (0, 2), (2, 2)],
    ]
    panel_rounds = [
        [[(0, 8), (1, 9)], [(0, 4), (1, 5)]],
        [[(0, 2), (1, 3), (4, 6), (5, 7), (8, 10), (9, 11)], [(8, 12), (9, 13), (4, 14), (5, 15)]],
    ]
    for pairs_list, offsets in zip(panel_rounds, corner_offsets[:2]):
        sent = panel
        for pairs in pairs_list:
            panel = panel + lax.ppermute(sent, "col", pairs)
            holders_col = holders_col + [dst for _, dst in pairs]
        corner, holders_k = spread_round(corner, holders_k, offsets, ncols)
    assert sorted(holders_col) == list(range(ncols))
    corner, panel = lax.optimization_barrier((corner, panel))
    corner, holders_k = spread_round(corner, holders_k, corner_offsets[2], ncols)
    assert len(holders_k) == nrows * ncols
    corner, panel_held = lax.optimization_barrier((corner, panel))

    lin = lambda r, c: r * ncols + c
    first_pairs = [(lin(c, r), lin(r, c)) for r in range(half) for c in range(ncols)]
    first_pairs += [(lin(c + half, r - half), lin(r, c)) for r in range(half, nrows) for c in range(ncols)]
    second_pairs = [(lin(c, r - half), lin(r, c)) for r in range(half, nrows) for c in range(ncols)]
    second_pairs += [(lin(c + half, r), lin(r, c)) for r in range(half) for c in range(ncols)]
    first = both_axes(panel, first_pairs)
    second = both_axes(panel, second_pairs)

    a00, a10, a11 = unpack_corner(corner)
    lead_block = jnp.concatenate(
        [jnp.concatenate([a00, a10.T], axis=1), jnp.concatenate([a10, a11], axis=1)], axis=0
    )
    factor = jnp.linalg.cholesky(lead_block)
    inv_t = lower_inverse(factor).T
    c0 = factor[:NB, :NB]
    c1 = factor[NB:, NB:]
    w_rows = mm(panel_held, inv_t)
    x_rows = w_rows[:, :NB]
    y_rows = w_rows[:, NB:]
    v = mm(w_rows, inv_t.T)
    zero_block = jnp.zeros((NB, NB), jnp.float32)

    low = p < half
    near = jnp.where(low, first, second)
    far = jnp.where(low, second, first)
    cols = interleave(near, far, row_count)
    update = mm(v, cols.T)

    row_ids = jnp.arange(row_count * NB, dtype=jnp.int32) // NB * nrows + p
    col_ids = jnp.arange(col_count * NB, dtype=jnp.int32) // NB * ncols + q
    keep = (col_ids[None, :] >= 2) & (row_ids[:, None] >= col_ids[None, :])
    result = jnp.where(keep, stored - update, 0.0)

    lead0 = jnp.concatenate([jnp.where(p == 0, c0, x_rows[:NB]), x_rows[NB:]], axis=0)
    lead1_top = jnp.where(p == 0, zero_block, jnp.where(p == 1, c1, y_rows[:NB]))
    lead1 = jnp.concatenate([lead1_top, y_rows[NB:]], axis=0)
    lead = jnp.where(q == 0, lead0, lead1)
    head = jnp.where(q < 2, lead, result[:, :NB])
    return jnp.concatenate([head, result[:, NB:]], axis=1)


def solution(mesh):
    return jax.shard_map(
        per_device,
        mesh=mesh,
        in_specs=(P("row", "col"),),
        out_specs=P("row", "col"),
        check_vma=False,
    )
```

```python
import jax
import jax.numpy as jnp
from jax import lax
from jax.sharding import PartitionSpec as P

NB = 64
HIGH = lax.Precision.HIGHEST


def both_axes(x, pairs):
    return lax.ppermute(x, ("row", "col"), pairs)


def mm(a, b):
    return jnp.dot(a, b, precision=HIGH, preferred_element_type=jnp.float32)


def gather_corner(stored, swapped, p, q, ncols):
    own = stored[:NB, :NB]
    got = swapped[:NB]
    d00, d01, d10, d11 = 0, 1, ncols, ncols + 1
    from_a = both_axes(own, [(d11, d00), (d00, d10)])
    from_b = both_axes(own, [(d11, d01), (d00, d11)])
    sent = jnp.where(q == 0, from_a, from_b)
    t = jnp.where(q == 0, got, own)
    u = jnp.where(q == 0, own, got)
    a00 = jnp.where(p == 0, u, sent)
    a10 = jnp.where(p == 0, t.T, u)
    a11 = jnp.where(p == 0, sent, t)
    return pack_corner(a00, a10, a11)


def pack_corner(a00, a10, a11):
    r = lax.broadcasted_iota(jnp.int32, (NB, NB), 0)
    c = lax.broadcasted_iota(jnp.int32, (NB, NB), 1)
    shared = jnp.where(r >= c, a00, a11)
    diag = jnp.sum(jnp.where(r == c, a11, 0.0), axis=0, keepdims=True)
    last = jnp.concatenate([diag, jnp.zeros((1, NB), jnp.float32)], axis=1)
    return jnp.concatenate([jnp.concatenate([shared, a10], axis=1), last], axis=0)


def unpack_corner(packed):
    r = lax.broadcasted_iota(jnp.int32, (NB, NB), 0)
    c = lax.broadcasted_iota(jnp.int32, (NB, NB), 1)
    shared = packed[:NB, :NB]
    a10 = packed[:NB, NB:]
    diag = packed[NB:, :NB]
    a00 = jnp.where(r >= c, shared, shared.T)
    a11 = jnp.where(r == c, diag, jnp.where(r < c, shared, shared.T))
    return a00, a10, a11


def spread_round(value, holders, offsets, ncols):
    grown = set(holders)
    total = value
    for dr, dc in offsets:
        pairs = [(r * ncols + c, (r + dr) * ncols + c + dc) for r, c in sorted(holders)]
        total = total + both_axes(value, pairs)
        grown.update((r + dr, c + dc) for r, c in holders)
    return total, grown


def interleave(a, b, count):
    width = a.shape[1]
    blocks = jnp.stack([a.reshape(count, NB, width), b.reshape(count, NB, width)], axis=1)
    return blocks.reshape(2 * count * NB, width)


def lower_inverse(factor):
    eye = jnp.eye(factor.shape[0], dtype=jnp.float32)
    return jax.scipy.linalg.solve_triangular(factor, eye, lower=True)


def per_device(stored):
    nrows = lax.axis_size("row")
    ncols = lax.axis_size("col")
    assert nrows == 2 * ncols and ncols == 16
    half = nrows // 2
    p = lax.axis_index("row")
    q = lax.axis_index("col")
    row_count = stored.shape[0] // NB
    col_count = stored.shape[1] // NB
    assert col_count == 2 * row_count
    rows_len = row_count * NB

    mine = stored[:, :NB]
    swapped = lax.ppermute(mine, "col", [(0, 1), (1, 0)])
    panel = jnp.concatenate(
        [jnp.where(q == 0, mine, swapped), jnp.where(q == 0, swapped, mine)], axis=1
    )
    panel = jnp.where(q < 2, panel, 0.0)
    corner = jnp.where((p < 2) & (q < 2), gather_corner(stored, swapped, p, q, ncols), 0.0)

    holders_col = [0, 1]
    holders_k = {(0, 0), (0, 1), (1, 0), (1, 1)}
    corner_offsets = [
        [(a * 16 + b * 8, c * 8) for a in (0, 1) for b in (0, 1) for c in (0, 1)][1:],
        [(4, 0), (0, 4), (4, 4)],
        [(2, 0), (0, 2), (2, 2)],
    ]
    panel_rounds = [
        [[(0, 8), (1, 9)], [(0, 4), (1, 5)]],
        [[(0, 2), (1, 3), (4, 6), (5, 7), (8, 10), (9, 11)], [(8, 12), (9, 13), (4, 14), (5, 15)]],
    ]
    for pairs_list, offsets in zip(panel_rounds, corner_offsets[:2]):
        sent = panel
        for pairs in pairs_list:
            panel = panel + lax.ppermute(sent, "col", pairs)
            holders_col = holders_col + [dst for _, dst in pairs]
        corner, holders_k = spread_round(corner, holders_k, offsets, ncols)
    assert sorted(holders_col) == list(range(ncols))
    corner, panel = lax.optimization_barrier((corner, panel))
    corner, holders_k = spread_round(corner, holders_k, corner_offsets[2], ncols)
    assert len(holders_k) == nrows * ncols
    corner, panel_held = lax.optimization_barrier((corner, panel))

    lin = lambda r, c: r * ncols + c
    first_pairs = [(lin(c, r), lin(r, c)) for r in range(half) for c in range(ncols)]
    first_pairs += [(lin(c + half, r - half), lin(r, c)) for r in range(half, nrows) for c in range(ncols)]
    second_pairs = [(lin(c, r - half), lin(r, c)) for r in range(half, nrows) for c in range(ncols)]
    second_pairs += [(lin(c + half, r), lin(r, c)) for r in range(half) for c in range(ncols)]
    first = both_axes(panel, first_pairs)
    second = both_axes(panel, second_pairs)

    a00, a10, a11 = unpack_corner(corner)
    lead_block = jnp.concatenate(
        [jnp.concatenate([a00, a10.T], axis=1), jnp.concatenate([a10, a11], axis=1)], axis=0
    )
    factor = jnp.linalg.cholesky(lead_block)
    inv_t = lower_inverse(factor).T
    c0 = factor[:NB, :NB]
    c1 = factor[NB:, NB:]
    w_rows = mm(panel_held, inv_t)
    x_rows = w_rows[:, :NB]
    y_rows = w_rows[:, NB:]
    v = mm(w_rows, inv_t.T)
    zero_block = jnp.zeros((NB, NB), jnp.float32)

    low = p < half
    near = jnp.where(low, first, second)
    far = jnp.where(low, second, first)
    cols = interleave(near, far, row_count)
    update = mm(v, cols.T)

    row_ids = jnp.arange(row_count * NB, dtype=jnp.int32) // NB * nrows + p
    col_ids = jnp.arange(col_count * NB, dtype=jnp.int32) // NB * ncols + q
    keep = (col_ids[None, :] >= 2) & (row_ids[:, None] >= col_ids[None, :])
    result = jnp.where(keep, stored - update, 0.0)

    lead0 = jnp.concatenate([jnp.where(p == 0, c0, x_rows[:NB]), x_rows[NB:]], axis=0)
    lead1_top = jnp.where(p == 0, zero_block, jnp.where(p == 1, c1, y_rows[:NB]))
    lead1 = jnp.concatenate([lead1_top, y_rows[NB:]], axis=0)
    lead = jnp.where(q == 0, lead0, lead1)
    lead_wide = jnp.pad(lead, ((0, 0), (0, (col_count - 1) * NB)))
    in_lead = (q < 2) & (jnp.arange(col_count * NB, dtype=jnp.int32)[None, :] < NB)
    return jnp.where(in_lead, lead_wide, result)


def solution(mesh):
    return jax.shard_map(
        per_device,
        mesh=mesh,
        in_specs=(P("row", "col"),),
        out_specs=P("row", "col"),
        check_vma=False,
    )
```

```python
import jax
import jax.numpy as jnp
from jax import lax
from jax.sharding import PartitionSpec as P

NB = 64
HIGH = lax.Precision.HIGHEST


def both_axes(x, pairs):
    return lax.ppermute(x, ("row", "col"), pairs)


def mm(a, b):
    return jnp.dot(a, b, precision=HIGH, preferred_element_type=jnp.float32)


def gather_corner(stored, swapped, p, q, ncols):
    own = stored[:NB, :NB]
    got = swapped[:NB]
    d00, d01, d10, d11 = 0, 1, ncols, ncols + 1
    from_a = both_axes(own, [(d11, d00), (d00, d10)])
    from_b = both_axes(own, [(d11, d01), (d00, d11)])
    sent = jnp.where(q == 0, from_a, from_b)
    t = jnp.where(q == 0, got, own)
    u = jnp.where(q == 0, own, got)
    a00 = jnp.where(p == 0, u, sent)
    a10 = jnp.where(p == 0, t.T, u)
    a11 = jnp.where(p == 0, sent, t)
    return pack_corner(a00, a10, a11)


def pack_corner(a00, a10, a11):
    r = lax.broadcasted_iota(jnp.int32, (NB, NB), 0)
    c = lax.broadcasted_iota(jnp.int32, (NB, NB), 1)
    shared = jnp.where(r >= c, a00, a11)
    diag = jnp.sum(jnp.where(r == c, a11, 0.0), axis=0, keepdims=True)
    last = jnp.concatenate([diag, jnp.zeros((1, NB), jnp.float32)], axis=1)
    return jnp.concatenate([jnp.concatenate([shared, a10], axis=1), last], axis=0)


def unpack_corner(packed):
    r = lax.broadcasted_iota(jnp.int32, (NB, NB), 0)
    c = lax.broadcasted_iota(jnp.int32, (NB, NB), 1)
    shared = packed[:NB, :NB]
    a10 = packed[:NB, NB:]
    diag = packed[NB:, :NB]
    a00 = jnp.where(r >= c, shared, shared.T)
    a11 = jnp.where(r == c, diag, jnp.where(r < c, shared, shared.T))
    return a00, a10, a11


def spread_round(value, holders, offsets, ncols):
    grown = set(holders)
    total = value
    for dr, dc in offsets:
        pairs = [(r * ncols + c, (r + dr) * ncols + c + dc) for r, c in sorted(holders)]
        total = total + both_axes(value, pairs)
        grown.update((r + dr, c + dc) for r, c in holders)
    return total, grown


def interleave(a, b, count):
    width = a.shape[1]
    blocks = jnp.stack([a.reshape(count, NB, width), b.reshape(count, NB, width)], axis=1)
    return blocks.reshape(2 * count * NB, width)


def lower_inverse(factor):
    eye = jnp.eye(factor.shape[0], dtype=jnp.float32)
    return jax.scipy.linalg.solve_triangular(factor, eye, lower=True)


def per_device(stored):
    nrows = lax.axis_size("row")
    ncols = lax.axis_size("col")
    assert nrows == 2 * ncols and ncols == 16
    half = nrows // 2
    p = lax.axis_index("row")
    q = lax.axis_index("col")
    row_count = stored.shape[0] // NB
    col_count = stored.shape[1] // NB
    assert col_count == 2 * row_count
    rows_len = row_count * NB

    mine = stored[:, :NB]
    swapped = lax.ppermute(mine, "col", [(0, 1), (1, 0)])
    panel = jnp.concatenate(
        [jnp.where(q == 0, mine, swapped), jnp.where(q == 0, swapped, mine)], axis=1
    )
    panel = jnp.where(q < 2, panel, 0.0)
    corner = jnp.where((p < 2) & (q < 2), gather_corner(stored, swapped, p, q, ncols), 0.0)

    holders_col = [0, 1]
    holders_k = {(0, 0), (0, 1), (1, 0), (1, 1)}
    corner_offsets = [
        [(a * 16 + b * 8, c * 8) for a in (0, 1) for b in (0, 1) for c in (0, 1)][1:],
        [(4, 0), (0, 4), (4, 4)],
        [(2, 0), (0, 2), (2, 2)],
    ]
    panel_rounds = [
        [[(0, 8), (1, 9)], [(0, 4), (1, 5)]],
        [[(0, 2), (1, 3), (4, 6), (5, 7), (8, 10), (9, 11)], [(8, 12), (9, 13), (4, 14), (5, 15)]],
    ]
    for pairs_list, offsets in zip(panel_rounds, corner_offsets[:2]):
        sent = panel
        for pairs in pairs_list:
            panel = panel + lax.ppermute(sent, "col", pairs)
            holders_col = holders_col + [dst for _, dst in pairs]
        corner, holders_k = spread_round(corner, holders_k, offsets, ncols)
    assert sorted(holders_col) == list(range(ncols))
    corner, panel = lax.optimization_barrier((corner, panel))
    corner, holders_k = spread_round(corner, holders_k, corner_offsets[2], ncols)
    assert len(holders_k) == nrows * ncols
    corner, panel_held = lax.optimization_barrier((corner, panel))

    lin = lambda r, c: r * ncols + c
    first_pairs = [(lin(c, r), lin(r, c)) for r in range(half) for c in range(ncols)]
    first_pairs += [(lin(c + half, r - half), lin(r, c)) for r in range(half, nrows) for c in range(ncols)]
    second_pairs = [(lin(c, r - half), lin(r, c)) for r in range(half, nrows) for c in range(ncols)]
    second_pairs += [(lin(c + half, r), lin(r, c)) for r in range(half) for c in range(ncols)]
    first = both_axes(panel, first_pairs)
    second = both_axes(panel, second_pairs)

    a00, a10, a11 = unpack_corner(corner)
    lead_block = jnp.concatenate(
        [jnp.concatenate([a00, a10.T], axis=1), jnp.concatenate([a10, a11], axis=1)], axis=0
    )
    factor = jnp.linalg.cholesky(lead_block, symmetrize_input=False)
    inv_t = lower_inverse(factor).T
    c0 = factor[:NB, :NB]
    c1 = factor[NB:, NB:]
    w_rows = mm(panel_held, inv_t)
    x_rows = w_rows[:, :NB]
    y_rows = w_rows[:, NB:]
    v = mm(w_rows, inv_t.T)
    zero_block = jnp.zeros((NB, NB), jnp.float32)

    low = p < half
    near = jnp.where(low, first, second)
    far = jnp.where(low, second, first)
    cols = interleave(near, far, row_count)
    update = mm(v, cols.T)

    row_ids = jnp.arange(row_count * NB, dtype=jnp.int32) // NB * nrows + p
    col_ids = jnp.arange(col_count * NB, dtype=jnp.int32) // NB * ncols + q
    keep = (col_ids[None, :] >= 2) & (row_ids[:, None] >= col_ids[None, :])
    result = jnp.where(keep, stored - update, 0.0)

    lead0 = jnp.concatenate([jnp.where(p == 0, c0, x_rows[:NB]), x_rows[NB:]], axis=0)
    lead1_top = jnp.where(p == 0, zero_block, jnp.where(p == 1, c1, y_rows[:NB]))
    lead1 = jnp.concatenate([lead1_top, y_rows[NB:]], axis=0)
    lead = jnp.where(q == 0, lead0, lead1)
    head = jnp.where(q < 2, lead, result[:, :NB])
    return jnp.concatenate([head, result[:, NB:]], axis=1)


def solution(mesh):
    return jax.shard_map(
        per_device,
        mesh=mesh,
        in_specs=(P("row", "col"),),
        out_specs=P("row", "col"),
        check_vma=False,
    )
```

```python
import jax
import jax.numpy as jnp
from jax import lax
from jax.sharding import PartitionSpec as P

NB = 64
HIGH = lax.Precision.HIGHEST


def both_axes(x, pairs):
    return lax.ppermute(x, ("row", "col"), pairs)


def mm(a, b):
    return jnp.dot(a, b, precision=HIGH, preferred_element_type=jnp.float32)


def gather_corner(stored, swapped, p, q, ncols):
    own = stored[:NB, :NB]
    got = swapped[:NB]
    d00, d01, d10, d11 = 0, 1, ncols, ncols + 1
    from_a = both_axes(own, [(d11, d00), (d00, d10)])
    from_b = both_axes(own, [(d11, d01), (d00, d11)])
    sent = jnp.where(q == 0, from_a, from_b)
    t = jnp.where(q == 0, got, own)
    u = jnp.where(q == 0, own, got)
    a00 = jnp.where(p == 0, u, sent)
    a10 = jnp.where(p == 0, t.T, u)
    a11 = jnp.where(p == 0, sent, t)
    return pack_corner(a00, a10, a11)


def pack_corner(a00, a10, a11):
    r = lax.broadcasted_iota(jnp.int32, (NB, NB), 0)
    c = lax.broadcasted_iota(jnp.int32, (NB, NB), 1)
    shared = jnp.where(r >= c, a00, a11)
    diag = jnp.sum(jnp.where(r == c, a11, 0.0), axis=0, keepdims=True)
    last = jnp.concatenate([diag, jnp.zeros((1, NB), jnp.float32)], axis=1)
    return jnp.concatenate([jnp.concatenate([shared, a10], axis=1), last], axis=0)


def unpack_corner(packed):
    r = lax.broadcasted_iota(jnp.int32, (NB, NB), 0)
    c = lax.broadcasted_iota(jnp.int32, (NB, NB), 1)
    shared = packed[:NB, :NB]
    a10 = packed[:NB, NB:]
    diag = packed[NB:, :NB]
    a00 = jnp.where(r >= c, shared, shared.T)
    a11 = jnp.where(r == c, diag, jnp.where(r < c, shared, shared.T))
    return a00, a10, a11


def spread_round(value, holders, offsets, ncols):
    grown = set(holders)
    total = value
    for dr, dc in offsets:
        pairs = [(r * ncols + c, (r + dr) * ncols + c + dc) for r, c in sorted(holders)]
        total = total + both_axes(value, pairs)
        grown.update((r + dr, c + dc) for r, c in holders)
    return total, grown


def interleave(a, b, count):
    width = a.shape[1]
    blocks = jnp.stack([a.reshape(count, NB, width), b.reshape(count, NB, width)], axis=1)
    return blocks.reshape(2 * count * NB, width)


def lower_inverse(factor):
    eye = jnp.eye(factor.shape[0], dtype=jnp.float32)
    return jax.scipy.linalg.solve_triangular(factor, eye, lower=True)


def per_device(stored):
    nrows = lax.axis_size("row")
    ncols = lax.axis_size("col")
    assert nrows == 2 * ncols and ncols == 16
    half = nrows // 2
    p = lax.axis_index("row")
    q = lax.axis_index("col")
    row_count = stored.shape[0] // NB
    col_count = stored.shape[1] // NB
    assert col_count == 2 * row_count
    rows_len = row_count * NB

    mine = stored[:, :NB]
    swapped = lax.ppermute(mine, "col", [(0, 1), (1, 0)])
    panel = jnp.concatenate(
        [jnp.where(q == 0, mine, swapped), jnp.where(q == 0, swapped, mine)], axis=1
    )
    panel = jnp.where(q < 2, panel, 0.0)
    corner = jnp.where((p < 2) & (q < 2), gather_corner(stored, swapped, p, q, ncols), 0.0)

    holders_col = [0, 1]
    holders_k = {(0, 0), (0, 1), (1, 0), (1, 1)}
    corner_offsets = [
        [(a * 16 + b * 8, c * 8) for a in (0, 1) for b in (0, 1) for c in (0, 1)][1:],
        [(4, 0), (0, 4), (4, 4)],
        [(2, 0), (0, 2), (2, 2)],
    ]
    panel_rounds = [
        [[(0, 8), (1, 9)], [(0, 4), (1, 5)]],
        [[(8, 12), (9, 13), (4, 14), (5, 15)], [(0, 2), (1, 3), (4, 6), (5, 7), (8, 10), (9, 11)]],
    ]
    for pairs_list, offsets in zip(panel_rounds, corner_offsets[:2]):
        sent = panel
        for pairs in pairs_list:
            panel = panel + lax.ppermute(sent, "col", pairs)
            holders_col = holders_col + [dst for _, dst in pairs]
        corner, holders_k = spread_round(corner, holders_k, offsets, ncols)
    assert sorted(holders_col) == list(range(ncols))
    corner, panel = lax.optimization_barrier((corner, panel))
    corner, holders_k = spread_round(corner, holders_k, corner_offsets[2], ncols)
    assert len(holders_k) == nrows * ncols
    corner, panel_held = lax.optimization_barrier((corner, panel))

    lin = lambda r, c: r * ncols + c
    first_pairs = [(lin(c, r), lin(r, c)) for r in range(half) for c in range(ncols)]
    first_pairs += [(lin(c + half, r - half), lin(r, c)) for r in range(half, nrows) for c in range(ncols)]
    second_pairs = [(lin(c, r - half), lin(r, c)) for r in range(half, nrows) for c in range(ncols)]
    second_pairs += [(lin(c + half, r), lin(r, c)) for r in range(half) for c in range(ncols)]
    first = both_axes(panel, first_pairs)
    second = both_axes(panel, second_pairs)

    a00, a10, a11 = unpack_corner(corner)
    lead_block = jnp.concatenate(
        [jnp.concatenate([a00, a10.T], axis=1), jnp.concatenate([a10, a11], axis=1)], axis=0
    )
    factor = jnp.linalg.cholesky(lead_block)
    inv_t = lower_inverse(factor).T
    c0 = factor[:NB, :NB]
    c1 = factor[NB:, NB:]
    w_rows = mm(panel_held, inv_t)
    x_rows = w_rows[:, :NB]
    y_rows = w_rows[:, NB:]
    v = mm(w_rows, inv_t.T)
    zero_block = jnp.zeros((NB, NB), jnp.float32)

    low = p < half
    near = jnp.where(low, first, second)
    far = jnp.where(low, second, first)
    cols = interleave(near, far, row_count)
    update = mm(v, cols.T)

    row_ids = jnp.arange(row_count * NB, dtype=jnp.int32) // NB * nrows + p
    col_ids = jnp.arange(col_count * NB, dtype=jnp.int32) // NB * ncols + q
    keep = (col_ids[None, :] >= 2) & (row_ids[:, None] >= col_ids[None, :])
    result = jnp.where(keep, stored - update, 0.0)

    lead0 = jnp.concatenate([jnp.where(p == 0, c0, x_rows[:NB]), x_rows[NB:]], axis=0)
    lead1_top = jnp.where(p == 0, zero_block, jnp.where(p == 1, c1, y_rows[:NB]))
    lead1 = jnp.concatenate([lead1_top, y_rows[NB:]], axis=0)
    lead = jnp.where(q == 0, lead0, lead1)
    head = jnp.where(q < 2, lead, result[:, :NB])
    return jnp.concatenate([head, result[:, NB:]], axis=1)


def solution(mesh):
    return jax.shard_map(
        per_device,
        mesh=mesh,
        in_specs=(P("row", "col"),),
        out_specs=P("row", "col"),
        check_vma=False,
    )
```

```python
import jax
import jax.numpy as jnp
from jax import lax
from jax.sharding import PartitionSpec as P

NB = 64
HIGH = lax.Precision.HIGHEST


def both_axes(x, pairs):
    return lax.ppermute(x, ("row", "col"), pairs)


def mm(a, b):
    return jnp.dot(a, b, precision=HIGH, preferred_element_type=jnp.float32)


def gather_corner(stored, swapped, p, q, ncols):
    own = stored[:NB, :NB]
    got = swapped[:NB]
    d00, d01, d10, d11 = 0, 1, ncols, ncols + 1
    from_a = both_axes(own, [(d11, d00), (d00, d10)])
    from_b = both_axes(own, [(d11, d01), (d00, d11)])
    sent = jnp.where(q == 0, from_a, from_b)
    t = jnp.where(q == 0, got, own)
    u = jnp.where(q == 0, own, got)
    a00 = jnp.where(p == 0, u, sent)
    a10 = jnp.where(p == 0, t.T, u)
    a11 = jnp.where(p == 0, sent, t)
    return pack_corner(a00, a10, a11)


def pack_corner(a00, a10, a11):
    r = lax.broadcasted_iota(jnp.int32, (NB, NB), 0)
    c = lax.broadcasted_iota(jnp.int32, (NB, NB), 1)
    shared = jnp.where(r >= c, a00, a11)
    diag = jnp.sum(jnp.where(r == c, a11, 0.0), axis=0, keepdims=True)
    last = jnp.concatenate([diag, jnp.zeros((1, NB), jnp.float32)], axis=1)
    return jnp.concatenate([jnp.concatenate([shared, a10], axis=1), last], axis=0)


def unpack_corner(packed):
    r = lax.broadcasted_iota(jnp.int32, (NB, NB), 0)
    c = lax.broadcasted_iota(jnp.int32, (NB, NB), 1)
    shared = packed[:NB, :NB]
    a10 = packed[:NB, NB:]
    diag = packed[NB:, :NB]
    a00 = jnp.where(r >= c, shared, shared.T)
    a11 = jnp.where(r == c, diag, jnp.where(r < c, shared, shared.T))
    return a00, a10, a11


def spread_round(value, holders, offsets, ncols):
    grown = set(holders)
    total = value
    for dr, dc in offsets:
        pairs = [(r * ncols + c, (r + dr) * ncols + c + dc) for r, c in sorted(holders)]
        total = total + both_axes(value, pairs)
        grown.update((r + dr, c + dc) for r, c in holders)
    return total, grown


def interleave(a, b, count):
    width = a.shape[1]
    blocks = jnp.stack([a.reshape(count, NB, width), b.reshape(count, NB, width)], axis=1)
    return blocks.reshape(2 * count * NB, width)


def lower_inverse(factor):
    eye = jnp.eye(factor.shape[0], dtype=jnp.float32)
    return jax.scipy.linalg.solve_triangular(factor, eye, lower=True)


def per_device(stored):
    nrows = lax.axis_size("row")
    ncols = lax.axis_size("col")
    assert nrows == 2 * ncols and ncols == 16
    half = nrows // 2
    p = lax.axis_index("row")
    q = lax.axis_index("col")
    row_count = stored.shape[0] // NB
    col_count = stored.shape[1] // NB
    assert col_count == 2 * row_count
    rows_len = row_count * NB

    mine = stored[:, :NB]
    swapped = lax.ppermute(mine, "col", [(0, 1), (1, 0)])
    panel = jnp.concatenate(
        [jnp.where(q == 0, mine, swapped), jnp.where(q == 0, swapped, mine)], axis=1
    )
    panel = jnp.where(q < 2, panel, 0.0)
    corner = jnp.where((p < 2) & (q < 2), gather_corner(stored, swapped, p, q, ncols), 0.0)

    holders_col = [0, 1]
    holders_k = {(0, 0), (0, 1), (1, 0), (1, 1)}
    corner_offsets = [
        [(a * 16 + b * 8, c * 8) for a in (0, 1) for b in (0, 1) for c in (0, 1)][:0:-1],
        [(4, 0), (0, 4), (4, 4)],
        [(2, 0), (0, 2), (2, 2)],
    ]
    panel_rounds = [
        [[(0, 8), (1, 9)], [(0, 4), (1, 5)]],
        [[(0, 2), (1, 3), (4, 6), (5, 7), (8, 10), (9, 11)], [(8, 12), (9, 13), (4, 14), (5, 15)]],
    ]
    for pairs_list, offsets in zip(panel_rounds, corner_offsets[:2]):
        sent = panel
        for pairs in pairs_list:
            panel = panel + lax.ppermute(sent, "col", pairs)
            holders_col = holders_col + [dst for _, dst in pairs]
        corner, holders_k = spread_round(corner, holders_k, offsets, ncols)
    assert sorted(holders_col) == list(range(ncols))
    corner, panel = lax.optimization_barrier((corner, panel))
    corner, holders_k = spread_round(corner, holders_k, corner_offsets[2], ncols)
    assert len(holders_k) == nrows * ncols
    corner, panel_held = lax.optimization_barrier((corner, panel))

    lin = lambda r, c: r * ncols + c
    first_pairs = [(lin(c, r), lin(r, c)) for r in range(half) for c in range(ncols)]
    first_pairs += [(lin(c + half, r - half), lin(r, c)) for r in range(half, nrows) for c in range(ncols)]
    second_pairs = [(lin(c, r - half), lin(r, c)) for r in range(half, nrows) for c in range(ncols)]
    second_pairs += [(lin(c + half, r), lin(r, c)) for r in range(half) for c in range(ncols)]
    first = both_axes(panel, first_pairs)
    second = both_axes(panel, second_pairs)

    a00, a10, a11 = unpack_corner(corner)
    lead_block = jnp.concatenate(
        [jnp.concatenate([a00, a10.T], axis=1), jnp.concatenate([a10, a11], axis=1)], axis=0
    )
    factor = jnp.linalg.cholesky(lead_block)
    inv_t = lower_inverse(factor).T
    c0 = factor[:NB, :NB]
    c1 = factor[NB:, NB:]
    w_rows = mm(panel_held, inv_t)
    x_rows = w_rows[:, :NB]
    y_rows = w_rows[:, NB:]
    v = mm(w_rows, inv_t.T)
    zero_block = jnp.zeros((NB, NB), jnp.float32)

    low = p < half
    near = jnp.where(low, first, second)
    far = jnp.where(low, second, first)
    cols = interleave(near, far, row_count)
    update = mm(v, cols.T)

    row_ids = jnp.arange(row_count * NB, dtype=jnp.int32) // NB * nrows + p
    col_ids = jnp.arange(col_count * NB, dtype=jnp.int32) // NB * ncols + q
    keep = (col_ids[None, :] >= 2) & (row_ids[:, None] >= col_ids[None, :])
    result = jnp.where(keep, stored - update, 0.0)

    lead0 = jnp.concatenate([jnp.where(p == 0, c0, x_rows[:NB]), x_rows[NB:]], axis=0)
    lead1_top = jnp.where(p == 0, zero_block, jnp.where(p == 1, c1, y_rows[:NB]))
    lead1 = jnp.concatenate([lead1_top, y_rows[NB:]], axis=0)
    lead = jnp.where(q == 0, lead0, lead1)
    head = jnp.where(q < 2, lead, result[:, :NB])
    return jnp.concatenate([head, result[:, NB:]], axis=1)


def solution(mesh):
    return jax.shard_map(
        per_device,
        mesh=mesh,
        in_specs=(P("row", "col"),),
        out_specs=P("row", "col"),
        check_vma=False,
    )
```
